256 devices in a mesh: ctx: 32 (over y, x, core), tp: 8 (over z).
Axes of the slice: x: 4, y: 4, z: 8, core: 2. Of those that a mesh axis runs over, the one named last changes fastest.
Arguments:
- queries: bfloat16 [8192, 4096], P('ctx', 'tp'), may hold values from -12 to 12, as said below
- key_rows: bfloat16 [8192, 1024], P('ctx', 'tp'), may hold values from -12 to 12, as said below
- value_rows: bfloat16 [8192, 1024], P('ctx', 'tp'), may hold values from -6 to 6
- segments: int32 [8192], replicated, may hold values from 0 to 63, never falling along the last dimension, each value on 1 to 4096 neighbouring positions
- owner_ids: int32 [8192, 1], P('ctx'), may hold values from 0 to 7; in each aligned block of 256 rows (0 to 255, 256 to 511, ...) at most 64 rows name the same one
- out_proj: bfloat16 [4096, 8192], P('tp'), may hold values from -0.09375 to 0.09375
- residual: bfloat16 [16384, 8192], P(('ctx', 'tp')), may hold values from -4 to 4
- norm_gain: float32 [8192], replicated, may hold values from 0.5 to 1.5
Outputs:
- hidden_out: bfloat16 [16384, 8192], P(('ctx', 'tp'))
- normed: bfloat16 [16384, 8192], P(('ctx', 'tp'))
The draws below stay inside these ranges and needn't reach their ends.
Inputs may be any that keep to these rules, and one draw needn't show every extreme that they name: `segments`: never falling along the tokens; every document has 1 to 4096 tokens and one has exactly 4096. `owner_ids`: among the rows of one device's token block no owner is named more than 64 times; some owner is named exactly 64 times in some block. `queries`: Real-valued entries. `key_rows`: Real-valued entries.
All inputs are finite; a program needn't handle non-finite values.
Results may differ from the reference program's by a relative error of at most 0.01.
Values may be sent and summed in bfloat16 or wider, within the bound.
No kernel may reach another device: no remote copies, remote signals or barrier semaphores. Data moves between devices by JAX's collectives and lax.ppermute only.
A program may use at most 128 MiB of HBM per device.

```python
import math
import jax
import jax.numpy as jnp
import numpy as np
from jax import lax

D = 8192
HEADS = 32
KV_HEADS = 8
HEAD_DIM = 128
TOK_DEV = 256
CAP = 64
TOKENS = 8192
SLOTS = 16384
DOCS = 64
DOC_MOST = 4096
N_CTX = 32
N_TP = 8


def shared_draw(key):
    base_key = jax.random.fold_in(key, 11)
    first_key, second_key = jax.random.split(base_key, 2)
    query_draw = jax.random.normal(first_key, (TOKENS, HEADS * HEAD_DIM), jnp.float32)
    key_draw = jax.random.normal(second_key, (TOKENS, KV_HEADS * HEAD_DIM), jnp.float32)
    return (query_draw, key_draw)


def draw_queries(key, part):
    return shared_draw(key)[0].astype(jnp.bfloat16)


def draw_key_rows(key, part):
    return shared_draw(key)[1].astype(jnp.bfloat16)


def block_scale(own_key, extent, pieces, low, high):
    level, own = 1.0, jax.random.fold_in(own_key, 6)
    for position, parts in pieces:
        steps = jnp.exp(jax.random.uniform(jax.random.fold_in(own, position), (parts,), jnp.float32, low / len(pieces), high / len(pieces)))
        level = level * jnp.repeat(steps, extent[position] // parts).reshape([-1 if axis == position else 1 for axis in range(len(extent))])
    return level


def length_profile(count, total, reach, slope):
    portions = [(1 << 20) // math.isqrt(standing ** slope) + 1 for standing in range(2, count + 1)]
    surplus, given = total - reach - (count - 1), [1] * (count - 1)
    while surplus > 0:
        movable = [i for i in range(count - 1) if given[i] < reach]
        mass, remaining = sum([portions[i] for i in movable]), surplus
        for i in movable:
            addition = min(reach - given[i], max(1, remaining * portions[i] // mass), surplus)
            given[i] = given[i] + addition
            surplus = surplus - addition
    return np.array([reach] + given)


def ragged_sizes(rng, count, total, most, lean):
    if count == 2:
        one = jax.random.randint(rng, (), max(1, total - most), min(most, total - 1) + 1)
        return jnp.stack([one, total - one])
    tallies = jnp.asarray(length_profile(count, total, most, lean), jnp.int32)
    twos = (count - 1) // 2
    donor, receiver = tallies[1:1 + 2 * twos:2], tallies[2:2 + 2 * twos:2]
    margin = jnp.minimum(donor - 1, most - receiver)
    moved = jax.random.randint(jax.random.fold_in(rng, 1), (twos,), 0, 1 << 20) % (margin + 1)
    tallies = tallies.at[1:1 + 2 * twos:2].set(donor - moved).at[2:2 + 2 * twos:2].set(receiver + moved)
    return tallies[jax.random.permutation(jax.random.fold_in(rng, 2), count)]


def assign_block(stream_key, own, number, rows, amount, top, most, lean):
    ranking = jax.random.permutation(stream_key, amount)
    packed, usual = portions_of(amount, rows * top, most, lean, True), portions_of(amount, rows * top, most, lean, False)
    places = jnp.arange(amount)

    def named(lengths, rotation):
        used = int((lengths > 0).sum())
        fixed = max(1, used // 4)
        passed = fixed + (places - fixed + rotation * (used - fixed)) % max(1, amount - fixed)
        return jnp.zeros((amount,), jnp.int32).at[ranking[jnp.where(places < fixed, places, passed)]].set(jnp.asarray(lengths, jnp.int32))

    lengths = jnp.where(number % 4 == 0, named(packed, number // 4), named(usual, number - number // 4 - 1))
    mixed = jax.random.permutation(jax.random.fold_in(own, 3), amount)
    source_of, taker = mixed[0:amount // 2 * 2:2], mixed[1:amount // 2 * 2:2]
    slack = jnp.minimum(lengths[source_of] - 1, most - lengths[taker]) // 2
    slack = jnp.where((source_of == ranking[0]) | (taker == ranking[0]) | (lengths[taker] == 0), 0, jnp.maximum(slack, 0))
    passed = jax.random.randint(jax.random.fold_in(own, 4), (amount // 2,), 0, 1 << 20) % (slack + 1)
    lengths = lengths.at[source_of].add(-passed).at[taker].add(passed)
    labels = jnp.searchsorted(jnp.cumsum(lengths), jnp.arange(rows * top), side="right").astype(jnp.int32)
    listing = labels.reshape(top, rows).T
    listing = listing[jax.random.permutation(jax.random.fold_in(own, 1), rows)]
    rotation = jax.random.randint(jax.random.fold_in(own, 2), (rows, 1), 0, top)
    return jnp.take_along_axis(listing, (jnp.arange(top)[None, :] + rotation) % top, axis=1)


def portions_of(number_of, total, limit, slope, full):
    loads = [(1 << 20) // math.isqrt(rank ** slope) + 1 for rank in range(1, number_of + 1)]
    largest = limit if full else min(limit, max(-(-total // number_of), total * loads[0] // sum(loads)))
    least = 1 if total - largest >= number_of - 1 else 0
    holding, surplus = [largest] + [least] * (number_of - 1), total - largest - least * (number_of - 1)
    while surplus > 0:
        free = [i for i in range(1, number_of) if holding[i] < largest] or [i for i in range(1, number_of) if holding[i] < limit]
        mass, budget = sum([loads[i] for i in free]), surplus
        for i in free:
            extra = min(limit - holding[i], max(1, budget * loads[i] // mass), surplus)
            holding[i] = holding[i] + extra
            surplus = surplus - extra
    return np.array(holding)


def centred(stream_key, dims, width, most, cuts=(), kind=jnp.bfloat16):
    result = jax.random.normal(stream_key, dims, jnp.float32) * width
    if len(cuts) > 0:
        result = block_scale(stream_key, dims, cuts, -0.22, 0.18) * result
    return jnp.clip(result, min=-most, max=most).astype(kind)


def setup_inputs(seed: int = 0) -> dict:
    arg_keys = jax.random.split(jax.random.key(seed), 9)
    queries = draw_queries(jax.random.fold_in(arg_keys[8], 71), 0)
    key_rows = draw_key_rows(jax.random.fold_in(arg_keys[8], 71), 0)
    value_rows = centred(arg_keys[2], (TOKENS, KV_HEADS * HEAD_DIM), 1.0, 6.0, ((0, 32), (1, 8)))
    segments = jnp.searchsorted(jnp.cumsum(ragged_sizes(arg_keys[3], DOCS, TOKENS, DOC_MOST, 2)), jnp.arange(TOKENS), side="right").astype(jnp.int32)
    owner_ids_keys = jax.random.split(jax.random.fold_in(arg_keys[4], 1), TOKENS // TOK_DEV)
    owner_ids_turns = jax.random.permutation(jax.random.fold_in(arg_keys[4], 3), TOKENS // TOK_DEV)
    owner_ids = jax.vmap(lambda own, number: assign_block(jax.random.fold_in(arg_keys[4], 2), own, number, TOK_DEV, N_TP, 1, CAP, 2))(owner_ids_keys, owner_ids_turns).reshape((TOKENS, 1))
    out_proj = centred(arg_keys[5], (HEADS * HEAD_DIM, D), (HEADS * HEAD_DIM) ** -0.5, 0.09375, ((0, 8),))
    residual = centred(arg_keys[6], (SLOTS, D), 0.5, 4.0, ((0, 256),))
    norm_gain = jnp.clip(1.0 + 0.1 * jax.random.normal(arg_keys[7], (D,), jnp.float32), 0.5, 1.5)
    return {"queries": queries, "key_rows": key_rows, "value_rows": value_rows, "segments": segments, "owner_ids": owner_ids, "out_proj": out_proj, "residual": residual, "norm_gain": norm_gain}


def reference(queries, key_rows, value_rows, segments, owner_ids, out_proj, residual, norm_gain):
    group_size = HEADS // KV_HEADS
    score_scale = 1.0 / math.sqrt(HEAD_DIM)
    key_all = key_rows.astype(jnp.float32).reshape(TOKENS, KV_HEADS, HEAD_DIM)
    value_all = value_rows.astype(jnp.float32).reshape(TOKENS, KV_HEADS, HEAD_DIM)
    block_rows = min(256, TOKENS)
    positions = jnp.arange(TOKENS, dtype=jnp.int32)

    def attend(block_index):
        first_row = (block_index * block_rows).astype(jnp.int32)
        query_block = lax.dynamic_slice_in_dim(queries, first_row, block_rows, 0).astype(jnp.float32)
        query_block = query_block.reshape(block_rows, KV_HEADS, group_size, HEAD_DIM)
        seg_block = lax.dynamic_slice_in_dim(segments, first_row, block_rows, 0)
        pos_block = first_row + jnp.arange(block_rows, dtype=jnp.int32)
        scores = jnp.einsum('tkgd,skd->kgts', query_block, key_all) * score_scale
        allowed = (seg_block[:, None] == segments[None, :]) & (positions[None, :] <= pos_block[:, None])
        scores = jnp.where(allowed, scores, -1e+30)
        running_max = lax.optimization_barrier(jnp.max(scores, axis=-1, keepdims=True))
        exponent = jnp.where(allowed, jnp.exp(scores - running_max), 0.0)
        totals = lax.optimization_barrier(jnp.sum(exponent, axis=-1))
        weights = exponent.astype(jnp.bfloat16).astype(jnp.float32)
        mixed_heads = jnp.einsum('kgts,skd->kgtd', weights, value_all) / totals[..., None]
        return jnp.transpose(mixed_heads, (2, 0, 1, 3)).reshape(block_rows, HEADS * HEAD_DIM).astype(jnp.bfloat16)
    attended = lax.map(attend, jnp.arange(TOKENS // block_rows, dtype=jnp.int32))
    attended = attended.reshape(TOKENS, HEADS * HEAD_DIM)
    shard_width = HEADS * HEAD_DIM // N_TP
    combined = jnp.zeros((TOKENS, D), jnp.float32)
    for shard_index in range(N_TP):
        lower = shard_index * shard_width
        partial_rows = jnp.dot(attended[:, lower:lower + shard_width], out_proj[lower:lower + shard_width], preferred_element_type=jnp.float32).astype(jnp.bfloat16)
        combined = combined + partial_rows.astype(jnp.float32)
    owners = owner_ids[:, 0]
    onehot = (owners[:, None] == jnp.arange(N_TP, dtype=jnp.int32)[None, :]).astype(jnp.int32)
    onehot = onehot.reshape(N_CTX, TOK_DEV, N_TP)
    before = jnp.cumsum(onehot, axis=1) - onehot
    row_rank = lax.optimization_barrier(jnp.sum(before * onehot, axis=2)).reshape(TOKENS)
    destination = (positions // TOK_DEV * N_TP + owners) * CAP + row_rank
    scattered = jnp.zeros((SLOTS, D), jnp.float32).at[destination].set(combined)
    hidden_sum = residual.astype(jnp.float32) + scattered
    mean_square = lax.optimization_barrier(jnp.mean(hidden_sum * hidden_sum, axis=-1, keepdims=True))
    normed = hidden_sum * lax.rsqrt(mean_square + 1e-05) * norm_gain.astype(jnp.float32)
    return (hidden_sum.astype(jnp.bfloat16), normed.astype(jnp.bfloat16))
```

```python
import math

import jax
import jax.numpy as jnp
from jax import lax
from jax.sharding import PartitionSpec as P

HEADS = 32
KV_HEADS = 8
HEAD_DIM = 128


def on_device(queries, key_rows, value_rows, segments, owner_ids, out_proj, residual, norm_gain):
    rows_here = queries.shape[0]
    kv_local = key_rows.shape[1] // HEAD_DIM
    kv_cols = kv_local * HEAD_DIM
    group_size = HEADS // KV_HEADS
    score_scale = 1.0 / math.sqrt(HEAD_DIM)
    my_block = lax.axis_index("ctx")
    my_start = my_block * rows_here
    query_heads = queries.reshape(rows_here, kv_local, group_size, HEAD_DIM)
    query_pos = my_start + jnp.arange(rows_here, dtype=jnp.int32)
    query_seg = lax.dynamic_slice_in_dim(segments, my_start, rows_here, 0)
    start_state = (
        jnp.full((kv_local, group_size, rows_here), -1e30, jnp.float32),
        jnp.zeros((kv_local, group_size, rows_here), jnp.float32),
        jnp.zeros((kv_local, group_size, rows_here, HEAD_DIM), jnp.float32),
    )
    kv_pair = jnp.concatenate([key_rows, value_rows], axis=1)
    kv_all = lax.all_gather(kv_pair, "ctx", axis=0, tiled=True)
    key_width = rows_here
    doc_start = jnp.sum((segments < query_seg[0]).astype(jnp.int32))
    first_block = doc_start // key_width

    def update(block_index, states):
        key_start = block_index * key_width
        kv_block = lax.dynamic_slice_in_dim(kv_all, key_start, key_width, 0)
        key_block = kv_block[:, :kv_cols].reshape(key_width, kv_local, HEAD_DIM)
        value_block = kv_block[:, kv_cols:].reshape(key_width, kv_local, HEAD_DIM)
        key_seg = lax.dynamic_slice_in_dim(segments, key_start, key_width, 0)
        key_pos = key_start + jnp.arange(key_width, dtype=jnp.int32)
        allowed = (query_seg[:, None] == key_seg[None, :]) & (
            key_pos[None, :] <= query_pos[:, None]
        )
        running_max, totals, weighted = states
        scores = (
            jnp.einsum("tkgd,skd->kgts", query_heads, key_block, preferred_element_type=jnp.float32)
            * score_scale
        )
        scores = jnp.where(allowed, scores, -1e30)
        new_max = jnp.maximum(running_max, jnp.max(scores, axis=-1))
        exponent = jnp.where(allowed, jnp.exp(scores - new_max[..., None]), 0.0)
        factor = jnp.exp(running_max - new_max)
        totals = totals * factor + jnp.sum(exponent, axis=-1)
        weighted = weighted * factor[..., None] + jnp.einsum(
            "kgts,skd->kgtd",
            exponent.astype(jnp.bfloat16),
            value_block,
            preferred_element_type=jnp.float32,
        )
        return (new_max, totals, weighted)

    running_max, totals, weighted = lax.fori_loop(first_block, my_block + 1, update, start_state)
    mixed_heads = weighted / totals[..., None]
    attended = jnp.transpose(mixed_heads, (2, 0, 1, 3)).reshape(rows_here, -1).astype(jnp.bfloat16)
    slot_count = residual.shape[0]
    owner_count = lax.axis_size("tp")
    owners = owner_ids[:, 0]
    onehot = (owners[:, None] == jnp.arange(owner_count, dtype=jnp.int32)[None, :]).astype(
        jnp.int32
    )
    before = jnp.cumsum(onehot, axis=0) - onehot
    row_rank = jnp.sum(before * onehot, axis=1)
    slot_of_token = owners * slot_count + row_rank
    all_slots = jnp.arange(owner_count * slot_count, dtype=jnp.int32)
    select = (slot_of_token[None, :] == all_slots[:, None]).astype(jnp.bfloat16)
    attended_slots = jnp.dot(select, attended, preferred_element_type=jnp.float32).astype(
        jnp.bfloat16
    )
    partial_slots = jnp.dot(attended_slots, out_proj, preferred_element_type=jnp.float32).astype(
        jnp.bfloat16
    )
    owned_rows = lax.psum_scatter(partial_slots, "tp", scatter_dimension=0, tiled=True).astype(
        jnp.float32
    )
    hidden_sum = residual.astype(jnp.float32) + owned_rows
    mean_square = jnp.mean(hidden_sum * hidden_sum, axis=-1, keepdims=True)
    normed = hidden_sum * lax.rsqrt(mean_square + 1e-05) * norm_gain
    return (hidden_sum.astype(jnp.bfloat16), normed.astype(jnp.bfloat16))


def solution(mesh):
    placed = (
        P("ctx", "tp"),
        P("ctx", "tp"),
        P("ctx", "tp"),
        P(),
        P("ctx", None),
        P("tp", None),
        P(("ctx", "tp"), None),
        P(),
    )
    return jax.shard_map(
        on_device,
        mesh=mesh,
        in_specs=placed,
        out_specs=(P(("ctx", "tp"), None), P(("ctx", "tp"), None)),
        check_vma=False,
    )
```

```python
import functools
import math

import jax
import jax.numpy as jnp
from jax import lax
from jax.experimental import pallas as pl
from jax.experimental.pallas import tpu as pltpu
from jax.sharding import PartitionSpec as P

HEADS = 32
KV_HEADS = 8
HEAD_DIM = 128
DOC_MOST = 4096


def attention_kernel(
    block_info, q_ref, kv_ref, qseg_ref, kseg_ref, out_ref, max_ref, total_ref, acc_ref, *, window, group
):
    step = pl.program_id(0)
    my_block = block_info[0]
    first_block = block_info[1]
    key_block = my_block - (window - 1) + step
    rows = q_ref.shape[0]
    key_width = kv_ref.shape[0]
    local_heads = acc_ref.shape[0]
    kv_cols = kv_ref.shape[1] // 2
    score_scale = 1.0 / math.sqrt(HEAD_DIM)

    @pl.when(step == 0)
    def _():
        max_ref[...] = jnp.full(max_ref.shape, -1e30, jnp.float32)
        total_ref[...] = jnp.zeros(total_ref.shape, jnp.float32)
        acc_ref[...] = jnp.zeros(acc_ref.shape, jnp.float32)

    @pl.when(key_block >= first_block)
    def _():
        query_pos = my_block * rows + lax.broadcasted_iota(jnp.int32, (rows, 1), 0)
        key_pos = key_block * key_width + lax.broadcasted_iota(jnp.int32, (1, key_width), 1)
        allowed = (qseg_ref[...] == kseg_ref[...]) & (key_pos <= query_pos)
        for head in range(local_heads):
            kv_head = head // group
            keys = kv_ref[:, kv_head * HEAD_DIM:(kv_head + 1) * HEAD_DIM]
            values = kv_ref[:, kv_cols + kv_head * HEAD_DIM:kv_cols + (kv_head + 1) * HEAD_DIM]
            query = q_ref[:, head * HEAD_DIM:(head + 1) * HEAD_DIM]
            scores = (
                lax.dot_general(
                    query, keys, (((1,), (1,)), ((), ())), preferred_element_type=jnp.float32
                )
                * score_scale
            )
            scores = jnp.where(allowed, scores, -1e30)
            running_max = max_ref[head]
            new_max = jnp.maximum(running_max, jnp.max(scores, axis=-1, keepdims=True))
            exponent = jnp.where(allowed, jnp.exp(scores - new_max), 0.0)
            factor = jnp.exp(running_max - new_max)
            total_ref[head] = total_ref[head] * factor + jnp.sum(exponent, axis=-1, keepdims=True)
            acc_ref[head] = acc_ref[head] * factor + jnp.dot(
                exponent.astype(jnp.bfloat16), values, preferred_element_type=jnp.float32
            )
            max_ref[head] = new_max

    @pl.when(step == window - 1)
    def _():
        for head in range(local_heads):
            out_ref[:, head * HEAD_DIM:(head + 1) * HEAD_DIM] = (
                acc_ref[head] / total_ref[head]
            ).astype(out_ref.dtype)


def attend_window(queries, kv_all, query_seg, segments, my_block, first_block, group):
    rows, q_cols = queries.shape
    key_width = rows
    block_count = kv_all.shape[0] // key_width
    window = min(block_count, DOC_MOST // key_width + 1)
    local_heads = q_cols // HEAD_DIM
    block_info = jnp.stack([my_block, first_block]).astype(jnp.int32)

    def kv_map(step, info):
        return (jnp.maximum(info[0] - (window - 1) + step, info[1]), 0)

    def kseg_map(step, info):
        return (0, jnp.maximum(info[0] - (window - 1) + step, info[1]))

    grid_spec = pltpu.PrefetchScalarGridSpec(
        num_scalar_prefetch=1,
        grid=(window,),
        in_specs=[
            pl.BlockSpec((rows, q_cols), lambda step, info: (0, 0)),
            pl.BlockSpec((key_width, kv_all.shape[1]), kv_map),
            pl.BlockSpec((rows, 1), lambda step, info: (0, 0)),
            pl.BlockSpec((1, key_width), kseg_map),
        ],
        out_specs=pl.BlockSpec((rows, q_cols), lambda step, info: (0, 0)),
        scratch_shapes=[
            pltpu.VMEM((local_heads, rows, 1), jnp.float32),
            pltpu.VMEM((local_heads, rows, 1), jnp.float32),
            pltpu.VMEM((local_heads, rows, HEAD_DIM), jnp.float32),
        ],
    )
    kernel = pl.pallas_call(
        functools.partial(attention_kernel, window=window, group=group),
        grid_spec=grid_spec,
        out_shape=jax.ShapeDtypeStruct((rows, q_cols), jnp.bfloat16),
        compiler_params=pltpu.CompilerParams(dimension_semantics=("arbitrary",)),
    )
    return kernel(
        block_info, queries, kv_all, query_seg.reshape(rows, 1), segments.reshape(1, -1)
    )


def on_device(queries, key_rows, value_rows, segments, owner_ids, out_proj, residual, norm_gain):
    rows_here = queries.shape[0]
    kv_local = key_rows.shape[1] // HEAD_DIM
    kv_cols = kv_local * HEAD_DIM
    group_size = HEADS // KV_HEADS
    score_scale = 1.0 / math.sqrt(HEAD_DIM)
    my_block = lax.axis_index("ctx")
    my_start = my_block * rows_here
    query_heads = queries.reshape(rows_here, kv_local, group_size, HEAD_DIM)
    query_pos = my_start + jnp.arange(rows_here, dtype=jnp.int32)
    query_seg = lax.dynamic_slice_in_dim(segments, my_start, rows_here, 0)
    kv_pair = jnp.concatenate([key_rows, value_rows], axis=1)
    kv_all = lax.all_gather(kv_pair, "ctx", axis=0, tiled=True)
    doc_start = jnp.sum((segments < query_seg[0]).astype(jnp.int32))
    first_block = doc_start // rows_here
    attended = attend_window(queries, kv_all, query_seg, segments, my_block, first_block, group_size)
    slot_count = residual.shape[0]
    owner_count = lax.axis_size("tp")
    owners = owner_ids[:, 0]
    onehot = (owners[:, None] == jnp.arange(owner_count, dtype=jnp.int32)[None, :]).astype(
        jnp.int32
    )
    before = jnp.cumsum(onehot, axis=0) - onehot
    row_rank = jnp.sum(before * onehot, axis=1)
    slot_of_token = owners * slot_count + row_rank
    all_slots = jnp.arange(owner_count * slot_count, dtype=jnp.int32)
    select = (slot_of_token[None, :] == all_slots[:, None]).astype(jnp.bfloat16)
    attended_slots = jnp.dot(select, attended, preferred_element_type=jnp.float32).astype(
        jnp.bfloat16
    )
    partial_slots = jnp.dot(attended_slots, out_proj, preferred_element_type=jnp.float32).astype(
        jnp.bfloat16
    )
    owned_rows = lax.psum_scatter(partial_slots, "tp", scatter_dimension=0, tiled=True).astype(
        jnp.float32
    )
    hidden_sum = residual.astype(jnp.float32) + owned_rows
    mean_square = jnp.mean(hidden_sum * hidden_sum, axis=-1, keepdims=True)
    normed = hidden_sum * lax.rsqrt(mean_square + 1e-05) * norm_gain
    return (hidden_sum.astype(jnp.bfloat16), normed.astype(jnp.bfloat16))


def solution(mesh):
    placed = (
        P("ctx", "tp"),
        P("ctx", "tp"),
        P("ctx", "tp"),
        P(),
        P("ctx", None),
        P("tp", None),
        P(("ctx", "tp"), None),
        P(),
    )
    return jax.shard_map(
        on_device,
        mesh=mesh,
        in_specs=placed,
        out_specs=(P(("ctx", "tp"), None), P(("ctx", "tp"), None)),
        check_vma=False,
    )
```

```python
import functools
import math

import jax
import jax.numpy as jnp
from jax import lax
from jax.experimental import pallas as pl
from jax.experimental.pallas import tpu as pltpu
from jax.sharding import PartitionSpec as P

HEADS = 32
KV_HEADS = 8
HEAD_DIM = 128
DOC_MOST = 4096


def attention_kernel(
    block_info, q_ref, kv_ref, qseg_ref, kseg_ref, out_ref, max_ref, total_ref, acc_ref, *, window, group
):
    step = pl.program_id(0)
    my_block = block_info[0]
    first_block = block_info[1]
    key_block = my_block - (window - 1) + step
    rows = q_ref.shape[0]
    key_width = kv_ref.shape[0]
    local_heads = acc_ref.shape[0]
    kv_cols = kv_ref.shape[1] // 2
    score_scale = 1.0 / math.sqrt(HEAD_DIM)

    @pl.when(step == 0)
    def _():
        max_ref[...] = jnp.full(max_ref.shape, -1e30, jnp.float32)
        total_ref[...] = jnp.zeros(total_ref.shape, jnp.float32)
        acc_ref[...] = jnp.zeros(acc_ref.shape, jnp.float32)

    @pl.when(key_block >= first_block)
    def _():
        query_pos = my_block * rows + lax.broadcasted_iota(jnp.int32, (rows, 1), 0)
        key_pos = key_block * key_width + lax.broadcasted_iota(jnp.int32, (1, key_width), 1)
        allowed = (qseg_ref[...] == kseg_ref[...]) & (key_pos <= query_pos)
        for head in range(local_heads):
            kv_head = head // group
            keys = kv_ref[:, kv_head * HEAD_DIM:(kv_head + 1) * HEAD_DIM]
            values = kv_ref[:, kv_cols + kv_head * HEAD_DIM:kv_cols + (kv_head + 1) * HEAD_DIM]
            query = q_ref[:, head * HEAD_DIM:(head + 1) * HEAD_DIM]
            scores = (
                lax.dot_general(
                    query, keys, (((1,), (1,)), ((), ())), preferred_element_type=jnp.float32
                )
                * score_scale
            )
            scores = jnp.where(allowed, scores, -1e30)
            running_max = max_ref[head]
            new_max = jnp.maximum(running_max, jnp.max(scores, axis=-1, keepdims=True))
            exponent = jnp.where(allowed, jnp.exp(scores - new_max), 0.0)
            factor = jnp.exp(running_max - new_max)
            total_ref[head] = total_ref[head] * factor + jnp.sum(exponent, axis=-1, keepdims=True)
            acc_ref[head] = acc_ref[head] * factor + jnp.dot(
                exponent.astype(jnp.bfloat16), values, preferred_element_type=jnp.float32
            )
            max_ref[head] = new_max

    @pl.when(step == window - 1)
    def _():
        for head in range(local_heads):
            out_ref[:, head * HEAD_DIM:(head + 1) * HEAD_DIM] = (
                acc_ref[head] / total_ref[head]
            ).astype(out_ref.dtype)


def attend_window(queries, kv_all, query_seg, segments, my_block, first_block, group, window):
    rows, q_cols = queries.shape
    key_width = rows
    local_heads = q_cols // HEAD_DIM
    block_info = jnp.stack([my_block, first_block]).astype(jnp.int32)

    def kv_map(step, info):
        return (jnp.maximum(step, info[1] - info[0] + (window - 1)), 0)

    def kseg_map(step, info):
        return (0, jnp.maximum(info[0] - (window - 1) + step, info[1]))

    grid_spec = pltpu.PrefetchScalarGridSpec(
        num_scalar_prefetch=1,
        grid=(window,),
        in_specs=[
            pl.BlockSpec((rows, q_cols), lambda step, info: (0, 0)),
            pl.BlockSpec((key_width, kv_all.shape[1]), kv_map),
            pl.BlockSpec((rows, 1), lambda step, info: (0, 0)),
            pl.BlockSpec((1, key_width), kseg_map),
        ],
        out_specs=pl.BlockSpec((rows, q_cols), lambda step, info: (0, 0)),
        scratch_shapes=[
            pltpu.VMEM((local_heads, rows, 1), jnp.float32),
            pltpu.VMEM((local_heads, rows, 1), jnp.float32),
            pltpu.VMEM((local_heads, rows, HEAD_DIM), jnp.float32),
        ],
    )
    kernel = pl.pallas_call(
        functools.partial(attention_kernel, window=window, group=group),
        grid_spec=grid_spec,
        out_shape=jax.ShapeDtypeStruct((rows, q_cols), jnp.bfloat16),
        compiler_params=pltpu.CompilerParams(dimension_semantics=("arbitrary",)),
    )
    return kernel(
        block_info, queries, kv_all, query_seg.reshape(rows, 1), segments.reshape(1, -1)
    )


def on_device(queries, key_rows, value_rows, segments, owner_ids, out_proj, residual, norm_gain):
    rows_here = queries.shape[0]
    kv_local = key_rows.shape[1] // HEAD_DIM
    kv_cols = kv_local * HEAD_DIM
    group_size = HEADS // KV_HEADS
    score_scale = 1.0 / math.sqrt(HEAD_DIM)
    my_block = lax.axis_index("ctx")
    my_start = my_block * rows_here
    query_heads = queries.reshape(rows_here, kv_local, group_size, HEAD_DIM)
    query_pos = my_start + jnp.arange(rows_here, dtype=jnp.int32)
    query_seg = lax.dynamic_slice_in_dim(segments, my_start, rows_here, 0)
    kv_pair = jnp.concatenate([key_rows, value_rows], axis=1)
    block_total = lax.axis_size("ctx")
    window = min(block_total, DOC_MOST // rows_here + 1)
    pieces = []
    for distance in range(window - 1, 0, -1):
        pairs = [(source, source + distance) for source in range(block_total - distance)]
        pieces.append(lax.ppermute(kv_pair, "ctx", pairs))
    pieces.append(kv_pair)
    kv_window = jnp.concatenate(pieces, axis=0)
    doc_start = jnp.sum((segments < query_seg[0]).astype(jnp.int32))
    first_block = doc_start // rows_here
    first_block = jnp.maximum(first_block, my_block - (window - 1))
    attended = attend_window(
        queries, kv_window, query_seg, segments, my_block, first_block, group_size, window
    )
    slot_count = residual.shape[0]
    owner_count = lax.axis_size("tp")
    owners = owner_ids[:, 0]
    onehot = (owners[:, None] == jnp.arange(owner_count, dtype=jnp.int32)[None, :]).astype(
        jnp.int32
    )
    before = jnp.cumsum(onehot, axis=0) - onehot
    row_rank = jnp.sum(before * onehot, axis=1)
    slot_of_token = owners * slot_count + row_rank
    all_slots = jnp.arange(owner_count * slot_count, dtype=jnp.int32)
    select = (slot_of_token[None, :] == all_slots[:, None]).astype(jnp.bfloat16)
    attended_slots = jnp.dot(select, attended, preferred_element_type=jnp.float32).astype(
        jnp.bfloat16
    )
    partial_slots = jnp.dot(attended_slots, out_proj, preferred_element_type=jnp.float32).astype(
        jnp.bfloat16
    )
    owned_rows = lax.psum_scatter(partial_slots, "tp", scatter_dimension=0, tiled=True).astype(
        jnp.float32
    )
    hidden_sum = residual.astype(jnp.float32) + owned_rows
    mean_square = jnp.mean(hidden_sum * hidden_sum, axis=-1, keepdims=True)
    normed = hidden_sum * lax.rsqrt(mean_square + 1e-05) * norm_gain
    return (hidden_sum.astype(jnp.bfloat16), normed.astype(jnp.bfloat16))


def solution(mesh):
    placed = (
        P("ctx", "tp"),
        P("ctx", "tp"),
        P("ctx", "tp"),
        P(),
        P("ctx", None),
        P("tp", None),
        P(("ctx", "tp"), None),
        P(),
    )
    return jax.shard_map(
        on_device,
        mesh=mesh,
        in_specs=placed,
        out_specs=(P(("ctx", "tp"), None), P(("ctx", "tp"), None)),
        check_vma=False,
    )
```

```python
import functools
import math

import jax
import jax.numpy as jnp
from jax import lax
from jax.experimental import pallas as pl
from jax.experimental.pallas import tpu as pltpu
from jax.sharding import PartitionSpec as P

HEADS = 32
KV_HEADS = 8
HEAD_DIM = 128
DOC_MOST = 4096
CHIP_AXES = ("ctx_y", "ctx_x")
CORE_AXIS = "ctx_core"
CTX_AXES = CHIP_AXES + (CORE_AXIS,)


def attention_kernel(
    block_info, q_ref, kv_ref, qseg_ref, kseg_ref, out_ref, max_ref, total_ref, acc_ref, *, window, group
):
    step = pl.program_id(0)
    my_block = block_info[0]
    first_block = block_info[1]
    key_block = my_block - (window - 1) + step
    rows = q_ref.shape[0]
    key_width = kv_ref.shape[0]
    local_heads = acc_ref.shape[0]
    kv_cols = kv_ref.shape[1] // 2
    score_scale = 1.0 / math.sqrt(HEAD_DIM)

    @pl.when(step == 0)
    def _():
        max_ref[...] = jnp.full(max_ref.shape, -1e30, jnp.float32)
        total_ref[...] = jnp.zeros(total_ref.shape, jnp.float32)
        acc_ref[...] = jnp.zeros(acc_ref.shape, jnp.float32)

    @pl.when(key_block >= first_block)
    def _():
        query_pos = my_block * rows + lax.broadcasted_iota(jnp.int32, (rows, 1), 0)
        key_pos = key_block * key_width + lax.broadcasted_iota(jnp.int32, (1, key_width), 1)
        allowed = (qseg_ref[...] == kseg_ref[...]) & (key_pos <= query_pos)
        for head in range(local_heads):
            kv_head = head // group
            keys = kv_ref[:, kv_head * HEAD_DIM:(kv_head + 1) * HEAD_DIM]
            values = kv_ref[:, kv_cols + kv_head * HEAD_DIM:kv_cols + (kv_head + 1) * HEAD_DIM]
            query = q_ref[:, head * HEAD_DIM:(head + 1) * HEAD_DIM]
            scores = (
                lax.dot_general(
                    query, keys, (((1,), (1,)), ((), ())), preferred_element_type=jnp.float32
                )
                * score_scale
            )
            scores = jnp.where(allowed, scores, -1e30)
            running_max = max_ref[head]
            new_max = jnp.maximum(running_max, jnp.max(scores, axis=-1, keepdims=True))
            exponent = jnp.where(allowed, jnp.exp(scores - new_max), 0.0)
            factor = jnp.exp(running_max - new_max)
            total_ref[head] = total_ref[head] * factor + jnp.sum(exponent, axis=-1, keepdims=True)
            acc_ref[head] = acc_ref[head] * factor + jnp.dot(
                exponent.astype(jnp.bfloat16), values, preferred_element_type=jnp.float32
            )
            max_ref[head] = new_max

    @pl.when(step == window - 1)
    def _():
        for head in range(local_heads):
            out_ref[:, head * HEAD_DIM:(head + 1) * HEAD_DIM] = (
                acc_ref[head] / total_ref[head]
            ).astype(out_ref.dtype)


def attend_window(queries, kv_all, query_seg, segments, my_block, first_block, group):
    rows, q_cols = queries.shape
    key_width = rows
    block_count = kv_all.shape[0] // key_width
    window = min(block_count, DOC_MOST // key_width + 1)
    local_heads = q_cols // HEAD_DIM
    block_info = jnp.stack([my_block, first_block]).astype(jnp.int32)

    def kv_map(step, info):
        return (jnp.maximum(info[0] - (window - 1) + step, info[1]), 0)

    def kseg_map(step, info):
        return (0, jnp.maximum(info[0] - (window - 1) + step, info[1]))

    grid_spec = pltpu.PrefetchScalarGridSpec(
        num_scalar_prefetch=1,
        grid=(window,),
        in_specs=[
            pl.BlockSpec((rows, q_cols), lambda step, info: (0, 0)),
            pl.BlockSpec((key_width, kv_all.shape[1]), kv_map),
            pl.BlockSpec((rows, 1), lambda step, info: (0, 0)),
            pl.BlockSpec((1, key_width), kseg_map),
        ],
        out_specs=pl.BlockSpec((rows, q_cols), lambda step, info: (0, 0)),
        scratch_shapes=[
            pltpu.VMEM((local_heads, rows, 1), jnp.float32),
            pltpu.VMEM((local_heads, rows, 1), jnp.float32),
            pltpu.VMEM((local_heads, rows, HEAD_DIM), jnp.float32),
        ],
    )
    kernel = pl.pallas_call(
        functools.partial(attention_kernel, window=window, group=group),
        grid_spec=grid_spec,
        out_shape=jax.ShapeDtypeStruct((rows, q_cols), jnp.bfloat16),
        compiler_params=pltpu.CompilerParams(dimension_semantics=("arbitrary",)),
    )
    return kernel(
        block_info, queries, kv_all, query_seg.reshape(rows, 1), segments.reshape(1, -1)
    )


def on_device(queries, key_rows, value_rows, segments, owner_ids, out_proj, residual, norm_gain):
    rows_here = queries.shape[0]
    kv_local = key_rows.shape[1] // HEAD_DIM
    kv_cols = kv_local * HEAD_DIM
    group_size = HEADS // KV_HEADS
    score_scale = 1.0 / math.sqrt(HEAD_DIM)
    my_block = lax.axis_index(CTX_AXES)
    my_start = my_block * rows_here
    query_heads = queries.reshape(rows_here, kv_local, group_size, HEAD_DIM)
    query_pos = my_start + jnp.arange(rows_here, dtype=jnp.int32)
    query_seg = lax.dynamic_slice_in_dim(segments, my_start, rows_here, 0)
    kv_pair = jnp.concatenate([key_rows, value_rows], axis=1)
    chip_pair = lax.all_gather(kv_pair, CORE_AXIS, axis=0, tiled=True)
    core = lax.axis_index(CORE_AXIS)
    half = lax.dynamic_slice_in_dim(chip_pair, core * kv_cols, kv_cols, 1)
    half_all = lax.all_gather(half, CHIP_AXES, axis=0, tiled=True)
    both = lax.all_gather(half_all, CORE_AXIS, axis=1, tiled=True)
    kv_all = both
    doc_start = jnp.sum((segments < query_seg[0]).astype(jnp.int32))
    first_block = doc_start // rows_here
    attended = attend_window(queries, kv_all, query_seg, segments, my_block, first_block, group_size)
    slot_count = residual.shape[0]
    owner_count = lax.axis_size("tp")
    owners = owner_ids[:, 0]
    onehot = (owners[:, None] == jnp.arange(owner_count, dtype=jnp.int32)[None, :]).astype(
        jnp.int32
    )
    before = jnp.cumsum(onehot, axis=0) - onehot
    row_rank = jnp.sum(before * onehot, axis=1)
    slot_of_token = owners * slot_count + row_rank
    all_slots = jnp.arange(owner_count * slot_count, dtype=jnp.int32)
    select = (slot_of_token[None, :] == all_slots[:, None]).astype(jnp.bfloat16)
    attended_slots = jnp.dot(select, attended, preferred_element_type=jnp.float32).astype(
        jnp.bfloat16
    )
    partial_slots = jnp.dot(attended_slots, out_proj, preferred_element_type=jnp.float32).astype(
        jnp.bfloat16
    )
    owned_rows = lax.psum_scatter(partial_slots, "tp", scatter_dimension=0, tiled=True).astype(
        jnp.float32
    )
    hidden_sum = residual.astype(jnp.float32) + owned_rows
    mean_square = jnp.mean(hidden_sum * hidden_sum, axis=-1, keepdims=True)
    normed = hidden_sum * lax.rsqrt(mean_square + 1e-05) * norm_gain
    return (hidden_sum.astype(jnp.bfloat16), normed.astype(jnp.bfloat16))


def solution(mesh):
    ctx_size = mesh.shape["ctx"]
    cores = 2 if ctx_size % 2 == 0 else 1
    chips = ctx_size // cores
    rows_of_chips = math.isqrt(chips) if math.isqrt(chips) ** 2 == chips else 1
    split_shape = (rows_of_chips, chips // rows_of_chips, cores, mesh.shape["tp"])
    split_mesh = jax.sharding.Mesh(
        mesh.devices.reshape(split_shape), CTX_AXES + ("tp",)
    )
    placed = (
        P(CTX_AXES, "tp"),
        P(CTX_AXES, "tp"),
        P(CTX_AXES, "tp"),
        P(),
        P(CTX_AXES, None),
        P("tp", None),
        P(CTX_AXES + ("tp",), None),
        P(),
    )
    return jax.shard_map(
        on_device,
        mesh=split_mesh,
        in_specs=placed,
        out_specs=(P(CTX_AXES + ("tp",), None), P(CTX_AXES + ("tp",), None)),
        check_vma=False,
    )
```

```python
import functools
import math

import jax
import jax.numpy as jnp
from jax import lax
from jax.experimental import pallas as pl
from jax.experimental.pallas import tpu as pltpu
from jax.sharding import PartitionSpec as P

HEADS = 32
KV_HEADS = 8
HEAD_DIM = 128
DOC_MOST = 4096


def attention_kernel(
    block_info, q_ref, kv_ref, qseg_ref, kseg_ref, out_ref, max_ref, total_ref, acc_ref, *, window, group
):
    step = pl.program_id(0)
    my_block = block_info[0]
    first_block = block_info[1]
    key_block = my_block - (window - 1) + step
    rows = q_ref.shape[0]
    key_width = kv_ref.shape[0]
    local_heads = acc_ref.shape[0]
    kv_cols = kv_ref.shape[1] // 2
    score_scale = 1.0 / math.sqrt(HEAD_DIM)

    @pl.when(step == 0)
    def _():
        max_ref[...] = jnp.full(max_ref.shape, -1e29, jnp.float32)
        total_ref[...] = jnp.zeros(total_ref.shape, jnp.float32)
        acc_ref[...] = jnp.zeros(acc_ref.shape, jnp.float32)

    def accumulate(masked):
        if masked:
            query_pos = my_block * rows + lax.broadcasted_iota(jnp.int32, (rows, 1), 0)
            key_pos = key_block * key_width + lax.broadcasted_iota(jnp.int32, (1, key_width), 1)
            allowed = (qseg_ref[...] == kseg_ref[...]) & (key_pos <= query_pos)
        for head in range(local_heads):
            kv_head = head // group
            keys = kv_ref[:, kv_head * HEAD_DIM:(kv_head + 1) * HEAD_DIM]
            values = kv_ref[:, kv_cols + kv_head * HEAD_DIM:kv_cols + (kv_head + 1) * HEAD_DIM]
            query = q_ref[:, head * HEAD_DIM:(head + 1) * HEAD_DIM]
            scores = (
                lax.dot_general(
                    query, keys, (((1,), (1,)), ((), ())), preferred_element_type=jnp.float32
                )
                * score_scale
            )
            if masked:
                scores = jnp.where(allowed, scores, -1e30)
            running_max = max_ref[head]
            new_max = jnp.maximum(running_max, jnp.max(scores, axis=-1, keepdims=True))
            exponent = jnp.exp(scores - new_max)
            factor = jnp.exp(running_max - new_max)
            total_ref[head] = total_ref[head] * factor + jnp.sum(exponent, axis=-1, keepdims=True)
            acc_ref[head] = acc_ref[head] * factor + jnp.dot(
                exponent.astype(jnp.bfloat16), values, preferred_element_type=jnp.float32
            )
            max_ref[head] = new_max

    active = key_block >= first_block
    whole = block_info[2 + step] == 1

    @pl.when(active & whole)
    def _():
        accumulate(False)

    @pl.when(active & jnp.logical_not(whole))
    def _():
        accumulate(True)

    @pl.when(step == window - 1)
    def _():
        for head in range(local_heads):
            out_ref[:, head * HEAD_DIM:(head + 1) * HEAD_DIM] = (
                acc_ref[head] / total_ref[head]
            ).astype(out_ref.dtype)


def attend_window(queries, kv_all, query_seg, segments, my_block, first_block, group):
    rows, q_cols = queries.shape
    key_width = rows
    block_count = kv_all.shape[0] // key_width
    window = min(block_count, DOC_MOST // key_width + 1)
    local_heads = q_cols // HEAD_DIM
    global_blocks = my_block - (window - 1) + jnp.arange(window, dtype=jnp.int32)
    clamped = jnp.clip(global_blocks, 0, segments.shape[0] // key_width - 1)
    key_first = segments[clamped * key_width]
    key_last = segments[clamped * key_width + key_width - 1]
    whole = (
        (key_first == key_last)
        & (key_first == query_seg[0])
        & (query_seg[0] == query_seg[rows - 1])
        & (global_blocks < my_block)
        & (global_blocks >= 0)
    )
    block_info = jnp.concatenate(
        [jnp.stack([my_block, first_block]), whole.astype(jnp.int32)]
    ).astype(jnp.int32)

    def kv_map(step, info):
        return (jnp.maximum(info[0] - (window - 1) + step, info[1]), 0)

    def kseg_map(step, info):
        return (0, jnp.maximum(info[0] - (window - 1) + step, info[1]))

    grid_spec = pltpu.PrefetchScalarGridSpec(
        num_scalar_prefetch=1,
        grid=(window,),
        in_specs=[
            pl.BlockSpec((rows, q_cols), lambda step, info: (0, 0)),
            pl.BlockSpec((key_width, kv_all.shape[1]), kv_map),
            pl.BlockSpec((rows, 1), lambda step, info: (0, 0)),
            pl.BlockSpec((1, key_width), kseg_map),
        ],
        out_specs=pl.BlockSpec((rows, q_cols), lambda step, info: (0, 0)),
        scratch_shapes=[
            pltpu.VMEM((local_heads, rows, 1), jnp.float32),
            pltpu.VMEM((local_heads, rows, 1), jnp.float32),
            pltpu.VMEM((local_heads, rows, HEAD_DIM), jnp.float32),
        ],
    )
    kernel = pl.pallas_call(
        functools.partial(attention_kernel, window=window, group=group),
        grid_spec=grid_spec,
        out_shape=jax.ShapeDtypeStruct((rows, q_cols), jnp.bfloat16),
        compiler_params=pltpu.CompilerParams(dimension_semantics=("arbitrary",)),
    )
    return kernel(
        block_info, queries, kv_all, query_seg.reshape(rows, 1), segments.reshape(1, -1)
    )


def on_device(queries, key_rows, value_rows, segments, owner_ids, out_proj, residual, norm_gain):
    rows_here = queries.shape[0]
    kv_local = key_rows.shape[1] // HEAD_DIM
    kv_cols = kv_local * HEAD_DIM
    group_size = HEADS // KV_HEADS
    score_scale = 1.0 / math.sqrt(HEAD_DIM)
    my_block = lax.axis_index("ctx")
    my_start = my_block * rows_here
    query_heads = queries.reshape(rows_here, kv_local, group_size, HEAD_DIM)
    query_pos = my_start + jnp.arange(rows_here, dtype=jnp.int32)
    query_seg = lax.dynamic_slice_in_dim(segments, my_start, rows_here, 0)
    kv_pair = jnp.concatenate([key_rows, value_rows], axis=1)
    kv_all = lax.all_gather(kv_pair, "ctx", axis=0, tiled=True)
    doc_start = jnp.sum((segments < query_seg[0]).astype(jnp.int32))
    first_block = doc_start // rows_here
    attended = attend_window(queries, kv_all, query_seg, segments, my_block, first_block, group_size)
    slot_count = residual.shape[0]
    owner_count = lax.axis_size("tp")
    owners = owner_ids[:, 0]
    onehot = (owners[:, None] == jnp.arange(owner_count, dtype=jnp.int32)[None, :]).astype(
        jnp.int32
    )
    before = jnp.cumsum(onehot, axis=0) - onehot
    row_rank = jnp.sum(before * onehot, axis=1)
    slot_of_token = owners * slot_count + row_rank
    all_slots = jnp.arange(owner_count * slot_count, dtype=jnp.int32)
    select = (slot_of_token[None, :] == all_slots[:, None]).astype(jnp.bfloat16)
    attended_slots = jnp.dot(select, attended, preferred_element_type=jnp.float32).astype(
        jnp.bfloat16
    )
    partial_slots = jnp.dot(attended_slots, out_proj, preferred_element_type=jnp.float32).astype(
        jnp.bfloat16
    )
    owned_rows = lax.psum_scatter(partial_slots, "tp", scatter_dimension=0, tiled=True).astype(
        jnp.float32
    )
    hidden_sum = residual.astype(jnp.float32) + owned_rows
    mean_square = jnp.mean(hidden_sum * hidden_sum, axis=-1, keepdims=True)
    normed = hidden_sum * lax.rsqrt(mean_square + 1e-05) * norm_gain
    return (hidden_sum.astype(jnp.bfloat16), normed.astype(jnp.bfloat16))


def solution(mesh):
    placed = (
        P("ctx", "tp"),
        P("ctx", "tp"),
        P("ctx", "tp"),
        P(),
        P("ctx", None),
        P("tp", None),
        P(("ctx", "tp"), None),
        P(),
    )
    return jax.shard_map(
        on_device,
        mesh=mesh,
        in_specs=placed,
        out_specs=(P(("ctx", "tp"), None), P(("ctx", "tp"), None)),
        check_vma=False,
    )
```

```python
import functools
import math

import jax
import jax.numpy as jnp
from jax import lax
from jax.experimental import pallas as pl
from jax.experimental.pallas import tpu as pltpu
from jax.sharding import PartitionSpec as P

HEADS = 32
KV_HEADS = 8
HEAD_DIM = 128
DOC_MOST = 4096


def attention_kernel(
    block_info, q_ref, kv_ref, qseg_ref, kseg_ref, out_ref, max_ref, total_ref, acc_ref, *, window, group
):
    step = pl.program_id(0)
    my_block = block_info[0]
    first_block = block_info[1]
    key_block = my_block - (window - 1) + step
    rows = q_ref.shape[0]
    key_width = kv_ref.shape[0]
    local_heads = acc_ref.shape[0]
    kv_cols = kv_ref.shape[1] // 2
    score_scale = 1.0 / math.sqrt(HEAD_DIM)

    @pl.when(step == 0)
    def _():
        max_ref[...] = jnp.full(max_ref.shape, -1e29, jnp.float32)
        total_ref[...] = jnp.zeros(total_ref.shape, jnp.float32)
        acc_ref[...] = jnp.zeros(acc_ref.shape, jnp.float32)

    def accumulate(masked):
        if masked:
            query_pos = block_info[2] + lax.broadcasted_iota(jnp.int32, (rows, 1), 0)
            key_pos = key_block * key_width + lax.broadcasted_iota(jnp.int32, (1, key_width), 1)
            allowed = (qseg_ref[...] == kseg_ref[...]) & (key_pos <= query_pos)
        for head in range(local_heads):
            kv_head = head // group
            keys = kv_ref[:, kv_head * HEAD_DIM:(kv_head + 1) * HEAD_DIM]
            values = kv_ref[:, kv_cols + kv_head * HEAD_DIM:kv_cols + (kv_head + 1) * HEAD_DIM]
            query = q_ref[:, head * HEAD_DIM:(head + 1) * HEAD_DIM]
            scores = (
                lax.dot_general(
                    query, keys, (((1,), (1,)), ((), ())), preferred_element_type=jnp.float32
                )
                * score_scale
            )
            if masked:
                scores = jnp.where(allowed, scores, -1e30)
            running_max = max_ref[head]
            new_max = jnp.maximum(running_max, jnp.max(scores, axis=-1, keepdims=True))
            exponent = jnp.exp(scores - new_max)
            factor = jnp.exp(running_max - new_max)
            total_ref[head] = total_ref[head] * factor + jnp.sum(exponent, axis=-1, keepdims=True)
            acc_ref[head] = acc_ref[head] * factor + jnp.dot(
                exponent.astype(jnp.bfloat16), values, preferred_element_type=jnp.float32
            )
            max_ref[head] = new_max

    active = key_block >= first_block
    whole = block_info[3 + step] == 1

    @pl.when(active & whole)
    def _():
        accumulate(False)

    @pl.when(active & jnp.logical_not(whole))
    def _():
        accumulate(True)

    @pl.when(step == window - 1)
    def _():
        for head in range(local_heads):
            out_ref[:, head * HEAD_DIM:(head + 1) * HEAD_DIM] = (
                acc_ref[head] / total_ref[head]
            ).astype(out_ref.dtype)


def attend_window(
    queries, kv_all, query_seg, segments, my_block, first_block, group, query_start, key_width
):
    rows, q_cols = queries.shape
    block_count = kv_all.shape[0] // key_width
    window = min(block_count, DOC_MOST // key_width + 1)
    local_heads = q_cols // HEAD_DIM
    global_blocks = my_block - (window - 1) + jnp.arange(window, dtype=jnp.int32)
    clamped = jnp.clip(global_blocks, 0, segments.shape[0] // key_width - 1)
    key_first = segments[clamped * key_width]
    key_last = segments[clamped * key_width + key_width - 1]
    whole = (
        (key_first == key_last)
        & (key_first == query_seg[0])
        & (query_seg[0] == query_seg[rows - 1])
        & (global_blocks < my_block)
        & (global_blocks >= 0)
    )
    block_info = jnp.concatenate(
        [jnp.stack([my_block, first_block, query_start]), whole.astype(jnp.int32)]
    ).astype(jnp.int32)

    def kv_map(step, info):
        return (jnp.maximum(info[0] - (window - 1) + step, info[1]), 0)

    def kseg_map(step, info):
        return (0, jnp.maximum(info[0] - (window - 1) + step, info[1]))

    grid_spec = pltpu.PrefetchScalarGridSpec(
        num_scalar_prefetch=1,
        grid=(window,),
        in_specs=[
            pl.BlockSpec((rows, q_cols), lambda step, info: (0, 0)),
            pl.BlockSpec((key_width, kv_all.shape[1]), kv_map),
            pl.BlockSpec((rows, 1), lambda step, info: (0, 0)),
            pl.BlockSpec((1, key_width), kseg_map),
        ],
        out_specs=pl.BlockSpec((rows, q_cols), lambda step, info: (0, 0)),
        scratch_shapes=[
            pltpu.VMEM((local_heads, rows, 1), jnp.float32),
            pltpu.VMEM((local_heads, rows, 1), jnp.float32),
            pltpu.VMEM((local_heads, rows, HEAD_DIM), jnp.float32),
        ],
    )
    kernel = pl.pallas_call(
        functools.partial(attention_kernel, window=window, group=group),
        grid_spec=grid_spec,
        out_shape=jax.ShapeDtypeStruct((rows, q_cols), jnp.bfloat16),
        compiler_params=pltpu.CompilerParams(dimension_semantics=("arbitrary",)),
    )
    return kernel(
        block_info, queries, kv_all, query_seg.reshape(rows, 1), segments.reshape(1, -1)
    )


def on_device(queries, key_rows, value_rows, segments, owner_ids, out_proj, residual, norm_gain):
    rows_here = queries.shape[0]
    kv_local = key_rows.shape[1] // HEAD_DIM
    kv_cols = kv_local * HEAD_DIM
    group_size = HEADS // KV_HEADS
    score_scale = 1.0 / math.sqrt(HEAD_DIM)
    my_block = lax.axis_index("ctx")
    my_start = my_block * rows_here
    query_heads = queries.reshape(rows_here, kv_local, group_size, HEAD_DIM)
    query_pos = my_start + jnp.arange(rows_here, dtype=jnp.int32)
    query_seg = lax.dynamic_slice_in_dim(segments, my_start, rows_here, 0)
    kv_pair = jnp.concatenate([key_rows, value_rows], axis=1)
    kv_all = lax.all_gather(kv_pair, "ctx", axis=0, tiled=True)
    slot_count = residual.shape[0]
    owner_count = lax.axis_size("tp")
    owners = owner_ids[:, 0]
    onehot = (owners[:, None] == jnp.arange(owner_count, dtype=jnp.int32)[None, :]).astype(
        jnp.int32
    )
    before = jnp.cumsum(onehot, axis=0) - onehot
    row_rank = jnp.sum(before * onehot, axis=1)
    slot_of_token = owners * slot_count + row_rank
    my_slots = lax.axis_index("tp") * slot_count + jnp.arange(slot_count, dtype=jnp.int32)
    select = (slot_of_token[None, :] == my_slots[:, None]).astype(jnp.bfloat16)
    halves = 2
    half_rows = rows_here // halves
    summed_parts = []
    for part in range(halves):
        part_rows = slice(part * half_rows, (part + 1) * half_rows)
        part_seg = query_seg[part_rows]
        doc_start = jnp.sum((segments < part_seg[0]).astype(jnp.int32))
        first_block = doc_start // rows_here
        attended = attend_window(
            queries[part_rows],
            kv_all,
            part_seg,
            segments,
            my_block,
            first_block,
            group_size,
            my_start + part * half_rows,
            rows_here,
        )
        partial_rows = jnp.dot(attended, out_proj, preferred_element_type=jnp.float32).astype(
            jnp.bfloat16
        )
        if summed_parts:
            partial_rows, _ = lax.optimization_barrier((partial_rows, summed_parts[-1]))
        summed_parts.append(lax.psum(partial_rows, "tp"))
    summed = jnp.concatenate(summed_parts, axis=0)
    owned_rows = jnp.dot(select, summed, preferred_element_type=jnp.float32)
    hidden_sum = residual.astype(jnp.float32) + owned_rows
    mean_square = jnp.mean(hidden_sum * hidden_sum, axis=-1, keepdims=True)
    normed = hidden_sum * lax.rsqrt(mean_square + 1e-05) * norm_gain
    return (hidden_sum.astype(jnp.bfloat16), normed.astype(jnp.bfloat16))


def solution(mesh):
    placed = (
        P("ctx", "tp"),
        P("ctx", "tp"),
        P("ctx", "tp"),
        P(),
        P("ctx", None),
        P("tp", None),
        P(("ctx", "tp"), None),
        P(),
    )
    return jax.shard_map(
        on_device,
        mesh=mesh,
        in_specs=placed,
        out_specs=(P(("ctx", "tp"), None), P(("ctx", "tp"), None)),
        check_vma=False,
    )
```

```python
import functools
import math

import jax
import jax.numpy as jnp
from jax import lax
from jax.experimental import pallas as pl
from jax.experimental.pallas import tpu as pltpu
from jax.sharding import PartitionSpec as P

HEADS = 32
KV_HEADS = 8
HEAD_DIM = 128
DOC_MOST = 4096


def attention_kernel(
    block_info,
    qt_ref,
    k_ref,
    vt_ref,
    qseg_ref,
    kseg_ref,
    out_ref,
    max_ref,
    total_ref,
    acc_ref,
    *,
    window,
    group,
):
    step = pl.program_id(0)
    my_block = block_info[0]
    first_block = block_info[1]
    key_block = my_block - (window - 1) + step
    rows = qt_ref.shape[1]
    key_width = k_ref.shape[0]
    local_heads = acc_ref.shape[0]
    score_scale = 1.0 / math.sqrt(HEAD_DIM)

    @pl.when(step == 0)
    def _():
        max_ref[...] = jnp.full(max_ref.shape, -1e29, jnp.float32)
        total_ref[...] = jnp.zeros(total_ref.shape, jnp.float32)
        acc_ref[...] = jnp.zeros(acc_ref.shape, jnp.float32)

    def accumulate(masked):
        if masked:
            query_pos = block_info[2] + lax.broadcasted_iota(jnp.int32, (1, rows), 1)
            key_pos = key_block * key_width + lax.broadcasted_iota(jnp.int32, (key_width, 1), 0)
            allowed = (kseg_ref[...] == qseg_ref[...]) & (key_pos <= query_pos)
        for head in range(local_heads):
            kv_head = head // group
            keys = k_ref[:, kv_head * HEAD_DIM:(kv_head + 1) * HEAD_DIM]
            values_t = vt_ref[kv_head * HEAD_DIM:(kv_head + 1) * HEAD_DIM, :]
            query_t = qt_ref[head * HEAD_DIM:(head + 1) * HEAD_DIM, :]
            scores = jnp.dot(keys, query_t, preferred_element_type=jnp.float32) * score_scale
            if masked:
                scores = jnp.where(allowed, scores, -1e30)
            running_max = max_ref[head]
            new_max = jnp.maximum(running_max, jnp.max(scores, axis=0, keepdims=True))
            exponent = jnp.exp(scores - new_max)
            factor = jnp.exp(running_max - new_max)
            total_ref[head] = total_ref[head] * factor + jnp.sum(exponent, axis=0, keepdims=True)
            acc_ref[head] = acc_ref[head] * factor + jnp.dot(
                values_t, exponent.astype(jnp.bfloat16), preferred_element_type=jnp.float32
            )
            max_ref[head] = new_max

    active = key_block >= first_block
    whole = block_info[3 + step] == 1

    @pl.when(active & whole)
    def _():
        accumulate(False)

    @pl.when(active & jnp.logical_not(whole))
    def _():
        accumulate(True)

    @pl.when(step == window - 1)
    def _():
        for head in range(local_heads):
            out_ref[head * HEAD_DIM:(head + 1) * HEAD_DIM, :] = (
                acc_ref[head] / total_ref[head]
            ).astype(out_ref.dtype)


def attend_window(queries, kv_all, query_seg, segments, my_block, first_block, group):
    rows, q_cols = queries.shape
    key_width = rows
    block_count = kv_all.shape[0] // key_width
    window = min(block_count, DOC_MOST // key_width + 1)
    local_heads = q_cols // HEAD_DIM
    kv_cols = kv_all.shape[1] // 2
    global_blocks = my_block - (window - 1) + jnp.arange(window, dtype=jnp.int32)
    clamped = jnp.clip(global_blocks, 0, block_count - 1)
    key_first = segments[clamped * key_width]
    key_last = segments[clamped * key_width + key_width - 1]
    whole = (
        (key_first == key_last)
        & (key_first == query_seg[0])
        & (query_seg[0] == query_seg[rows - 1])
        & (global_blocks < my_block)
        & (global_blocks >= 0)
    )
    block_info = jnp.concatenate(
        [jnp.stack([my_block, first_block, my_block * rows]), whole.astype(jnp.int32)]
    ).astype(jnp.int32)

    def key_index(step, info):
        return jnp.maximum(info[0] - (window - 1) + step, info[1])

    grid_spec = pltpu.PrefetchScalarGridSpec(
        num_scalar_prefetch=1,
        grid=(window,),
        in_specs=[
            pl.BlockSpec((q_cols, rows), lambda step, info: (0, 0)),
            pl.BlockSpec((key_width, kv_cols), lambda step, info: (key_index(step, info), 0)),
            pl.BlockSpec((kv_cols, key_width), lambda step, info: (0, key_index(step, info))),
            pl.BlockSpec((1, rows), lambda step, info: (0, 0)),
            pl.BlockSpec((key_width, 1), lambda step, info: (key_index(step, info), 0)),
        ],
        out_specs=pl.BlockSpec((q_cols, rows), lambda step, info: (0, 0)),
        scratch_shapes=[
            pltpu.VMEM((local_heads, 1, rows), jnp.float32),
            pltpu.VMEM((local_heads, 1, rows), jnp.float32),
            pltpu.VMEM((local_heads, HEAD_DIM, rows), jnp.float32),
        ],
    )
    kernel = pl.pallas_call(
        functools.partial(attention_kernel, window=window, group=group),
        grid_spec=grid_spec,
        out_shape=jax.ShapeDtypeStruct((q_cols, rows), jnp.bfloat16),
        compiler_params=pltpu.CompilerParams(dimension_semantics=("arbitrary",)),
    )
    attended_t = kernel(
        block_info,
        queries.T,
        kv_all,
        kv_all[:, kv_cols:].T,
        query_seg.reshape(1, rows),
        segments.reshape(-1, 1),
    )
    return attended_t.T


def on_device(queries, key_rows, value_rows, segments, owner_ids, out_proj, residual, norm_gain):
    rows_here = queries.shape[0]
    kv_local = key_rows.shape[1] // HEAD_DIM
    kv_cols = kv_local * HEAD_DIM
    group_size = HEADS // KV_HEADS
    score_scale = 1.0 / math.sqrt(HEAD_DIM)
    my_block = lax.axis_index("ctx")
    my_start = my_block * rows_here
    query_heads = queries.reshape(rows_here, kv_local, group_size, HEAD_DIM)
    query_pos = my_start + jnp.arange(rows_here, dtype=jnp.int32)
    query_seg = lax.dynamic_slice_in_dim(segments, my_start, rows_here, 0)
    kv_pair = jnp.concatenate([key_rows, value_rows], axis=1)
    kv_all = lax.all_gather(kv_pair, "ctx", axis=0, tiled=True)
    doc_start = jnp.sum((segments < query_seg[0]).astype(jnp.int32))
    first_block = doc_start // rows_here
    attended = attend_window(queries, kv_all, query_seg, segments, my_block, first_block, group_size)
    slot_count = residual.shape[0]
    owner_count = lax.axis_size("tp")
    owners = owner_ids[:, 0]
    onehot = (owners[:, None] == jnp.arange(owner_count, dtype=jnp.int32)[None, :]).astype(
        jnp.int32
    )
    before = jnp.cumsum(onehot, axis=0) - onehot
    row_rank = jnp.sum(before * onehot, axis=1)
    slot_of_token = owners * slot_count + row_rank
    all_slots = jnp.arange(owner_count * slot_count, dtype=jnp.int32)
    select = (slot_of_token[None, :] == all_slots[:, None]).astype(jnp.bfloat16)
    attended_slots = jnp.dot(select, attended, preferred_element_type=jnp.float32).astype(
        jnp.bfloat16
    )
    partial_slots = jnp.dot(attended_slots, out_proj, preferred_element_type=jnp.float32).astype(
        jnp.bfloat16
    )
    owned_rows = lax.psum_scatter(partial_slots, "tp", scatter_dimension=0, tiled=True).astype(
        jnp.float32
    )
    hidden_sum = residual.astype(jnp.float32) + owned_rows
    mean_square = jnp.mean(hidden_sum * hidden_sum, axis=-1, keepdims=True)
    normed = hidden_sum * lax.rsqrt(mean_square + 1e-05) * norm_gain
    return (hidden_sum.astype(jnp.bfloat16), normed.astype(jnp.bfloat16))


def solution(mesh):
    placed = (
        P("ctx", "tp"),
        P("ctx", "tp"),
        P("ctx", "tp"),
        P(),
        P("ctx", None),
        P("tp", None),
        P(("ctx", "tp"), None),
        P(),
    )
    return jax.shard_map(
        on_device,
        mesh=mesh,
        in_specs=placed,
        out_specs=(P(("ctx", "tp"), None), P(("ctx", "tp"), None)),
        check_vma=False,
    )
```

```python
import functools
import math

import jax
import jax.numpy as jnp
from jax import lax
from jax.experimental import pallas as pl
from jax.experimental.pallas import tpu as pltpu
from jax.sharding import PartitionSpec as P

HEADS = 32
KV_HEADS = 8
HEAD_DIM = 128
DOC_MOST = 4096


def attention_kernel(
    block_info,
    qt_ref,
    kv_ref,
    qseg_ref,
    kseg_ref,
    out_ref,
    max_ref,
    total_ref,
    acc_ref,
    *,
    window,
    group,
):
    step = pl.program_id(0)
    my_block = block_info[0]
    first_block = block_info[1]
    key_block = my_block - (window - 1) + step
    rows = qt_ref.shape[1]
    key_width = kv_ref.shape[0]
    local_heads = acc_ref.shape[0]
    kv_cols = kv_ref.shape[1] // 2
    score_scale = 1.0 / math.sqrt(HEAD_DIM)

    @pl.when(step == 0)
    def _():
        max_ref[...] = jnp.full(max_ref.shape, -1e29, jnp.float32)
        total_ref[...] = jnp.zeros(total_ref.shape, jnp.float32)
        acc_ref[...] = jnp.zeros(acc_ref.shape, jnp.float32)

    def accumulate(masked):
        if masked:
            query_pos = block_info[2] + lax.broadcasted_iota(jnp.int32, (1, rows), 1)
            key_pos = key_block * key_width + lax.broadcasted_iota(jnp.int32, (key_width, 1), 0)
            allowed = (kseg_ref[...] == qseg_ref[...]) & (key_pos <= query_pos)
        values_t = []
        for kv_head in range(local_heads // group):
            values = kv_ref[:, kv_cols + kv_head * HEAD_DIM:kv_cols + (kv_head + 1) * HEAD_DIM]
            values_t.append(values.astype(jnp.float32).T.astype(jnp.bfloat16))
        for head in range(local_heads):
            kv_head = head // group
            keys = kv_ref[:, kv_head * HEAD_DIM:(kv_head + 1) * HEAD_DIM]
            query_t = qt_ref[head * HEAD_DIM:(head + 1) * HEAD_DIM, :]
            scores = jnp.dot(keys, query_t, preferred_element_type=jnp.float32) * score_scale
            if masked:
                scores = jnp.where(allowed, scores, -1e30)
            running_max = max_ref[head]
            new_max = jnp.maximum(running_max, jnp.max(scores, axis=0, keepdims=True))
            exponent = jnp.exp(scores - new_max)
            factor = jnp.exp(running_max - new_max)
            total_ref[head] = total_ref[head] * factor + jnp.sum(exponent, axis=0, keepdims=True)
            acc_ref[head] = acc_ref[head] * factor + jnp.dot(
                values_t[kv_head], exponent.astype(jnp.bfloat16), preferred_element_type=jnp.float32
            )
            max_ref[head] = new_max

    active = key_block >= first_block
    whole = block_info[3 + step] == 1

    @pl.when(active & whole)
    def _():
        accumulate(False)

    @pl.when(active & jnp.logical_not(whole))
    def _():
        accumulate(True)

    @pl.when(step == window - 1)
    def _():
        for head in range(local_heads):
            out_ref[head * HEAD_DIM:(head + 1) * HEAD_DIM, :] = (
                acc_ref[head] / total_ref[head]
            ).astype(out_ref.dtype)


def attend_window(queries, kv_all, query_seg, segments, my_block, first_block, group):
    rows, q_cols = queries.shape
    key_width = rows
    block_count = kv_all.shape[0] // key_width
    window = min(block_count, DOC_MOST // key_width + 1)
    local_heads = q_cols // HEAD_DIM
    kv_cols = kv_all.shape[1] // 2
    global_blocks = my_block - (window - 1) + jnp.arange(window, dtype=jnp.int32)
    clamped = jnp.clip(global_blocks, 0, block_count - 1)
    key_first = segments[clamped * key_width]
    key_last = segments[clamped * key_width + key_width - 1]
    whole = (
        (key_first == key_last)
        & (key_first == query_seg[0])
        & (query_seg[0] == query_seg[rows - 1])
        & (global_blocks < my_block)
        & (global_blocks >= 0)
    )
    block_info = jnp.concatenate(
        [jnp.stack([my_block, first_block, my_block * rows]), whole.astype(jnp.int32)]
    ).astype(jnp.int32)

    def key_index(step, info):
        return jnp.maximum(info[0] - (window - 1) + step, info[1])

    grid_spec = pltpu.PrefetchScalarGridSpec(
        num_scalar_prefetch=1,
        grid=(window,),
        in_specs=[
            pl.BlockSpec((q_cols, rows), lambda step, info: (0, 0)),
            pl.BlockSpec((key_width, 2 * kv_cols), lambda step, info: (key_index(step, info), 0)),
            pl.BlockSpec((1, rows), lambda step, info: (0, 0)),
            pl.BlockSpec((key_width, 1), lambda step, info: (key_index(step, info), 0)),
        ],
        out_specs=pl.BlockSpec((q_cols, rows), lambda step, info: (0, 0)),
        scratch_shapes=[
            pltpu.VMEM((local_heads, 1, rows), jnp.float32),
            pltpu.VMEM((local_heads, 1, rows), jnp.float32),
            pltpu.VMEM((local_heads, HEAD_DIM, rows), jnp.float32),
        ],
    )
    kernel = pl.pallas_call(
        functools.partial(attention_kernel, window=window, group=group),
        grid_spec=grid_spec,
        out_shape=jax.ShapeDtypeStruct((q_cols, rows), jnp.bfloat16),
        compiler_params=pltpu.CompilerParams(dimension_semantics=("arbitrary",)),
    )
    attended_t = kernel(
        block_info,
        queries.T,
        kv_all,
        query_seg.reshape(1, rows),
        segments.reshape(-1, 1),
    )
    return attended_t.T


def on_device(queries, key_rows, value_rows, segments, owner_ids, out_proj, residual, norm_gain):
    rows_here = queries.shape[0]
    kv_local = key_rows.shape[1] // HEAD_DIM
    kv_cols = kv_local * HEAD_DIM
    group_size = HEADS // KV_HEADS
    score_scale = 1.0 / math.sqrt(HEAD_DIM)
    my_block = lax.axis_index("ctx")
    my_start = my_block * rows_here
    query_heads = queries.reshape(rows_here, kv_local, group_size, HEAD_DIM)
    query_pos = my_start + jnp.arange(rows_here, dtype=jnp.int32)
    query_seg = lax.dynamic_slice_in_dim(segments, my_start, rows_here, 0)
    kv_pair = jnp.concatenate([key_rows, value_rows], axis=1)
    kv_all = lax.all_gather(kv_pair, "ctx", axis=0, tiled=True)
    doc_start = jnp.sum((segments < query_seg[0]).astype(jnp.int32))
    first_block = doc_start // rows_here
    attended = attend_window(queries, kv_all, query_seg, segments, my_block, first_block, group_size)
    slot_count = residual.shape[0]
    owner_count = lax.axis_size("tp")
    owners = owner_ids[:, 0]
    onehot = (owners[:, None] == jnp.arange(owner_count, dtype=jnp.int32)[None, :]).astype(
        jnp.int32
    )
    before = jnp.cumsum(onehot, axis=0) - onehot
    row_rank = jnp.sum(before * onehot, axis=1)
    slot_of_token = owners * slot_count + row_rank
    all_slots = jnp.arange(owner_count * slot_count, dtype=jnp.int32)
    select = (slot_of_token[None, :] == all_slots[:, None]).astype(jnp.bfloat16)
    attended_slots = jnp.dot(select, attended, preferred_element_type=jnp.float32).astype(
        jnp.bfloat16
    )
    partial_slots = jnp.dot(attended_slots, out_proj, preferred_element_type=jnp.float32).astype(
        jnp.bfloat16
    )
    owned_rows = lax.psum_scatter(partial_slots, "tp", scatter_dimension=0, tiled=True).astype(
        jnp.float32
    )
    hidden_sum = residual.astype(jnp.float32) + owned_rows
    mean_square = jnp.mean(hidden_sum * hidden_sum, axis=-1, keepdims=True)
    normed = hidden_sum * lax.rsqrt(mean_square + 1e-05) * norm_gain
    return (hidden_sum.astype(jnp.bfloat16), normed.astype(jnp.bfloat16))


def solution(mesh):
    placed = (
        P("ctx", "tp"),
        P("ctx", "tp"),
        P("ctx", "tp"),
        P(),
        P("ctx", None),
        P("tp", None),
        P(("ctx", "tp"), None),
        P(),
    )
    return jax.shard_map(
        on_device,
        mesh=mesh,
        in_specs=placed,
        out_specs=(P(("ctx", "tp"), None), P(("ctx", "tp"), None)),
        check_vma=False,
    )
```

```python
import functools
import math

import jax
import jax.numpy as jnp
from jax import lax
from jax.experimental import pallas as pl
from jax.experimental.pallas import tpu as pltpu
from jax.sharding import PartitionSpec as P

HEADS = 32
KV_HEADS = 8
HEAD_DIM = 128
DOC_MOST = 4096


def attention_kernel(
    block_info,
    qt_ref,
    kv_ref,
    qseg_ref,
    kseg_ref,
    out_ref,
    max_ref,
    total_ref,
    acc_ref,
    *,
    window,
    group,
):
    step = pl.program_id(0)
    my_block = block_info[0]
    first_block = block_info[1]
    key_block = my_block - (window - 1) + step
    rows = qt_ref.shape[1] // group
    key_width = kv_ref.shape[0]
    local_heads = acc_ref.shape[0] * group
    kv_cols = kv_ref.shape[1] // 2
    score_scale = 1.0 / math.sqrt(HEAD_DIM)

    @pl.when(step == 0)
    def _():
        max_ref[...] = jnp.full(max_ref.shape, -1e29, jnp.float32)
        total_ref[...] = jnp.zeros(total_ref.shape, jnp.float32)
        acc_ref[...] = jnp.zeros(acc_ref.shape, jnp.float32)

    def accumulate(masked):
        if masked:
            lane = lax.broadcasted_iota(jnp.int32, (1, group * rows), 1)
            query_pos = block_info[2] + lane % rows
            key_pos = key_block * key_width + lax.broadcasted_iota(jnp.int32, (key_width, 1), 0)
            allowed = (kseg_ref[...] == qseg_ref[...]) & (key_pos <= query_pos)
        for kv_head in range(local_heads // group):
            keys = kv_ref[:, kv_head * HEAD_DIM:(kv_head + 1) * HEAD_DIM]
            values = kv_ref[:, kv_cols + kv_head * HEAD_DIM:kv_cols + (kv_head + 1) * HEAD_DIM]
            values_t = values.astype(jnp.float32).T.astype(jnp.bfloat16)
            query_t = qt_ref[kv_head * HEAD_DIM:(kv_head + 1) * HEAD_DIM, :]
            scores = jnp.dot(keys, query_t, preferred_element_type=jnp.float32) * score_scale
            if masked:
                scores = jnp.where(allowed, scores, -1e30)
            running_max = max_ref[kv_head]
            new_max = jnp.maximum(running_max, jnp.max(scores, axis=0, keepdims=True))
            exponent = jnp.exp(scores - new_max)
            factor = jnp.exp(running_max - new_max)
            total_ref[kv_head] = total_ref[kv_head] * factor + jnp.sum(
                exponent, axis=0, keepdims=True
            )
            acc_ref[kv_head] = acc_ref[kv_head] * factor + jnp.dot(
                values_t, exponent.astype(jnp.bfloat16), preferred_element_type=jnp.float32
            )
            max_ref[kv_head] = new_max

    active = key_block >= first_block
    whole = block_info[3 + step] == 1

    @pl.when(active & whole)
    def _():
        accumulate(False)

    @pl.when(active & jnp.logical_not(whole))
    def _():
        accumulate(True)

    @pl.when(step == window - 1)
    def _():
        for kv_head in range(local_heads // group):
            out_ref[kv_head * HEAD_DIM:(kv_head + 1) * HEAD_DIM, :] = (
                acc_ref[kv_head] / total_ref[kv_head]
            ).astype(out_ref.dtype)


def attend_window(queries, kv_all, query_seg, segments, my_block, first_block, group):
    rows, q_cols = queries.shape
    key_width = rows
    block_count = kv_all.shape[0] // key_width
    window = min(block_count, DOC_MOST // key_width + 1)
    local_heads = q_cols // HEAD_DIM
    kv_cols = kv_all.shape[1] // 2
    kv_local = local_heads // group
    queries_t = (
        queries.reshape(rows, kv_local, group, HEAD_DIM)
        .transpose(1, 3, 2, 0)
        .reshape(kv_local * HEAD_DIM, group * rows)
    )
    global_blocks = my_block - (window - 1) + jnp.arange(window, dtype=jnp.int32)
    clamped = jnp.clip(global_blocks, 0, block_count - 1)
    key_first = segments[clamped * key_width]
    key_last = segments[clamped * key_width + key_width - 1]
    whole = (
        (key_first == key_last)
        & (key_first == query_seg[0])
        & (query_seg[0] == query_seg[rows - 1])
        & (global_blocks < my_block)
        & (global_blocks >= 0)
    )
    block_info = jnp.concatenate(
        [jnp.stack([my_block, first_block, my_block * rows]), whole.astype(jnp.int32)]
    ).astype(jnp.int32)

    def key_index(step, info):
        return jnp.maximum(info[0] - (window - 1) + step, info[1])

    grid_spec = pltpu.PrefetchScalarGridSpec(
        num_scalar_prefetch=1,
        grid=(window,),
        in_specs=[
            pl.BlockSpec((kv_cols, group * rows), lambda step, info: (0, 0)),
            pl.BlockSpec((key_width, 2 * kv_cols), lambda step, info: (key_index(step, info), 0)),
            pl.BlockSpec((1, group * rows), lambda step, info: (0, 0)),
            pl.BlockSpec((key_width, 1), lambda step, info: (key_index(step, info), 0)),
        ],
        out_specs=pl.BlockSpec((kv_cols, group * rows), lambda step, info: (0, 0)),
        scratch_shapes=[
            pltpu.VMEM((kv_local, 1, group * rows), jnp.float32),
            pltpu.VMEM((kv_local, 1, group * rows), jnp.float32),
            pltpu.VMEM((kv_local, HEAD_DIM, group * rows), jnp.float32),
        ],
    )
    kernel = pl.pallas_call(
        functools.partial(attention_kernel, window=window, group=group),
        grid_spec=grid_spec,
        out_shape=jax.ShapeDtypeStruct((kv_cols, group * rows), jnp.bfloat16),
        compiler_params=pltpu.CompilerParams(dimension_semantics=("arbitrary",)),
    )
    attended_t = kernel(
        block_info,
        queries_t,
        kv_all,
        jnp.tile(query_seg, group).reshape(1, group * rows),
        segments.reshape(-1, 1),
    )
    return (
        attended_t.reshape(kv_local, HEAD_DIM, group, rows)
        .transpose(3, 0, 2, 1)
        .reshape(rows, q_cols)
    )


def on_device(queries, key_rows, value_rows, segments, owner_ids, out_proj, residual, norm_gain):
    rows_here = queries.shape[0]
    kv_local = key_rows.shape[1] // HEAD_DIM
    kv_cols = kv_local * HEAD_DIM
    group_size = HEADS // KV_HEADS
    score_scale = 1.0 / math.sqrt(HEAD_DIM)
    my_block = lax.axis_index("ctx")
    my_start = my_block * rows_here
    query_heads = queries.reshape(rows_here, kv_local, group_size, HEAD_DIM)
    query_pos = my_start + jnp.arange(rows_here, dtype=jnp.int32)
    query_seg = lax.dynamic_slice_in_dim(segments, my_start, rows_here, 0)
    kv_pair = jnp.concatenate([key_rows, value_rows], axis=1)
    kv_all = lax.all_gather(kv_pair, "ctx", axis=0, tiled=True)
    doc_start = jnp.sum((segments < query_seg[0]).astype(jnp.int32))
    first_block = doc_start // rows_here
    attended = attend_window(queries, kv_all, query_seg, segments, my_block, first_block, group_size)
    slot_count = residual.shape[0]
    owner_count = lax.axis_size("tp")
    owners = owner_ids[:, 0]
    onehot = (owners[:, None] == jnp.arange(owner_count, dtype=jnp.int32)[None, :]).astype(
        jnp.int32
    )
    before = jnp.cumsum(onehot, axis=0) - onehot
    row_rank = jnp.sum(before * onehot, axis=1)
    slot_of_token = owners * slot_count + row_rank
    all_slots = jnp.arange(owner_count * slot_count, dtype=jnp.int32)
    select = (slot_of_token[None, :] == all_slots[:, None]).astype(jnp.bfloat16)
    attended_slots = jnp.dot(select, attended, preferred_element_type=jnp.float32).astype(
        jnp.bfloat16
    )
    partial_slots = jnp.dot(attended_slots, out_proj, preferred_element_type=jnp.float32).astype(
        jnp.bfloat16
    )
    owned_rows = lax.psum_scatter(partial_slots, "tp", scatter_dimension=0, tiled=True).astype(
        jnp.float32
    )
    hidden_sum = residual.astype(jnp.float32) + owned_rows
    mean_square = jnp.mean(hidden_sum * hidden_sum, axis=-1, keepdims=True)
    normed = hidden_sum * lax.rsqrt(mean_square + 1e-05) * norm_gain
    return (hidden_sum.astype(jnp.bfloat16), normed.astype(jnp.bfloat16))


def solution(mesh):
    placed = (
        P("ctx", "tp"),
        P("ctx", "tp"),
        P("ctx", "tp"),
        P(),
        P("ctx", None),
        P("tp", None),
        P(("ctx", "tp"), None),
        P(),
    )
    return jax.shard_map(
        on_device,
        mesh=mesh,
        in_specs=placed,
        out_specs=(P(("ctx", "tp"), None), P(("ctx", "tp"), None)),
        check_vma=False,
    )
```

```python
import functools
import math

import jax
import jax.numpy as jnp
from jax import lax
from jax.experimental import pallas as pl
from jax.experimental.pallas import tpu as pltpu
from jax.sharding import PartitionSpec as P

HEADS = 32
KV_HEADS = 8
HEAD_DIM = 128
DOC_MOST = 4096


def attention_kernel(
    block_info,
    qt_ref,
    kv_ref,
    kv_next_ref,
    qseg_ref,
    kseg_ref,
    kseg_next_ref,
    out_ref,
    max_ref,
    total_ref,
    acc_ref,
    *,
    window,
    group,
):
    step = pl.program_id(0)
    my_block = block_info[0]
    first_block = block_info[1]
    steps = (window + 1) // 2
    rows = qt_ref.shape[1] // group
    key_width = kv_ref.shape[0]
    local_heads = acc_ref.shape[0] * group
    kv_cols = kv_ref.shape[1] // 2
    score_scale = 1.0 / math.sqrt(HEAD_DIM)

    @pl.when(step == 0)
    def _():
        max_ref[...] = jnp.full(max_ref.shape, -1e29, jnp.float32)
        total_ref[...] = jnp.zeros(total_ref.shape, jnp.float32)
        acc_ref[...] = jnp.zeros(acc_ref.shape, jnp.float32)

    def accumulate(masked, kv_ref, kseg_ref, key_block):
        if masked:
            lane = lax.broadcasted_iota(jnp.int32, (1, group * rows), 1)
            query_pos = block_info[2] + lane % rows
            key_pos = key_block * key_width + lax.broadcasted_iota(jnp.int32, (key_width, 1), 0)
            allowed = (kseg_ref[...] == qseg_ref[...]) & (key_pos <= query_pos)
        for kv_head in range(local_heads // group):
            keys = kv_ref[:, kv_head * HEAD_DIM:(kv_head + 1) * HEAD_DIM]
            values = kv_ref[:, kv_cols + kv_head * HEAD_DIM:kv_cols + (kv_head + 1) * HEAD_DIM]
            values_t = values.astype(jnp.float32).T.astype(jnp.bfloat16)
            query_t = qt_ref[kv_head * HEAD_DIM:(kv_head + 1) * HEAD_DIM, :]
            scores = jnp.dot(keys, query_t, preferred_element_type=jnp.float32) * score_scale
            if masked:
                scores = jnp.where(allowed, scores, -1e30)
            running_max = max_ref[kv_head]
            new_max = jnp.maximum(running_max, jnp.max(scores, axis=0, keepdims=True))
            exponent = jnp.exp(scores - new_max)
            factor = jnp.exp(running_max - new_max)
            total_ref[kv_head] = total_ref[kv_head] * factor + jnp.sum(
                exponent, axis=0, keepdims=True
            )
            acc_ref[kv_head] = acc_ref[kv_head] * factor + jnp.dot(
                values_t, exponent.astype(jnp.bfloat16), preferred_element_type=jnp.float32
            )
            max_ref[kv_head] = new_max

    for sub, (kv_sub, kseg_sub) in enumerate(((kv_ref, kseg_ref), (kv_next_ref, kseg_next_ref))):
        place = 2 * step + sub
        key_block = my_block - (window - 1) + place
        active = (key_block >= first_block) & (place < window)
        whole = block_info[3 + place] == 1

        @pl.when(active & whole)
        def _():
            accumulate(False, kv_sub, kseg_sub, key_block)

        @pl.when(active & jnp.logical_not(whole))
        def _():
            accumulate(True, kv_sub, kseg_sub, key_block)

    @pl.when(step == steps - 1)
    def _():
        for kv_head in range(local_heads // group):
            out_ref[kv_head * HEAD_DIM:(kv_head + 1) * HEAD_DIM, :] = (
                acc_ref[kv_head] / total_ref[kv_head]
            ).astype(out_ref.dtype)


def attend_window(queries, kv_all, query_seg, segments, my_block, first_block, group):
    rows, q_cols = queries.shape
    key_width = rows
    block_count = kv_all.shape[0] // key_width
    window = min(block_count, DOC_MOST // key_width + 1)
    local_heads = q_cols // HEAD_DIM
    kv_cols = kv_all.shape[1] // 2
    kv_local = local_heads // group
    queries_t = (
        queries.reshape(rows, kv_local, group, HEAD_DIM)
        .transpose(1, 3, 2, 0)
        .reshape(kv_local * HEAD_DIM, group * rows)
    )
    global_blocks = my_block - (window - 1) + jnp.arange(window, dtype=jnp.int32)
    clamped = jnp.clip(global_blocks, 0, block_count - 1)
    key_first = segments[clamped * key_width]
    key_last = segments[clamped * key_width + key_width - 1]
    whole = (
        (key_first == key_last)
        & (key_first == query_seg[0])
        & (query_seg[0] == query_seg[rows - 1])
        & (global_blocks < my_block)
        & (global_blocks >= 0)
    )
    steps = (window + 1) // 2
    block_info = jnp.concatenate(
        [
            jnp.stack([my_block, first_block, my_block * rows]),
            whole.astype(jnp.int32),
            jnp.zeros((2 * steps - window,), jnp.int32),
        ]
    ).astype(jnp.int32)

    def key_index(place, info):
        return jnp.minimum(jnp.maximum(info[0] - (window - 1) + place, info[1]), info[0])

    grid_spec = pltpu.PrefetchScalarGridSpec(
        num_scalar_prefetch=1,
        grid=(steps,),
        in_specs=[
            pl.BlockSpec((kv_cols, group * rows), lambda step, info: (0, 0)),
            pl.BlockSpec(
                (key_width, 2 * kv_cols), lambda step, info: (key_index(2 * step, info), 0)
            ),
            pl.BlockSpec(
                (key_width, 2 * kv_cols), lambda step, info: (key_index(2 * step + 1, info), 0)
            ),
            pl.BlockSpec((1, group * rows), lambda step, info: (0, 0)),
            pl.BlockSpec((key_width, 1), lambda step, info: (key_index(2 * step, info), 0)),
            pl.BlockSpec((key_width, 1), lambda step, info: (key_index(2 * step + 1, info), 0)),
        ],
        out_specs=pl.BlockSpec((kv_cols, group * rows), lambda step, info: (0, 0)),
        scratch_shapes=[
            pltpu.VMEM((kv_local, 1, group * rows), jnp.float32),
            pltpu.VMEM((kv_local, 1, group * rows), jnp.float32),
            pltpu.VMEM((kv_local, HEAD_DIM, group * rows), jnp.float32),
        ],
    )
    kernel = pl.pallas_call(
        functools.partial(attention_kernel, window=window, group=group),
        grid_spec=grid_spec,
        out_shape=jax.ShapeDtypeStruct((kv_cols, group * rows), jnp.bfloat16),
        compiler_params=pltpu.CompilerParams(dimension_semantics=("arbitrary",)),
    )
    attended_t = kernel(
        block_info,
        queries_t,
        kv_all,
        kv_all,
        jnp.tile(query_seg, group).reshape(1, group * rows),
        segments.reshape(-1, 1),
        segments.reshape(-1, 1),
    )
    return (
        attended_t.reshape(kv_local, HEAD_DIM, group, rows)
        .transpose(3, 0, 2, 1)
        .reshape(rows, q_cols)
    )


def on_device(queries, key_rows, value_rows, segments, owner_ids, out_proj, residual, norm_gain):
    rows_here = queries.shape[0]
    kv_local = key_rows.shape[1] // HEAD_DIM
    kv_cols = kv_local * HEAD_DIM
    group_size = HEADS // KV_HEADS
    score_scale = 1.0 / math.sqrt(HEAD_DIM)
    my_block = lax.axis_index("ctx")
    my_start = my_block * rows_here
    query_heads = queries.reshape(rows_here, kv_local, group_size, HEAD_DIM)
    query_pos = my_start + jnp.arange(rows_here, dtype=jnp.int32)
    query_seg = lax.dynamic_slice_in_dim(segments, my_start, rows_here, 0)
    kv_pair = jnp.concatenate([key_rows, value_rows], axis=1)
    kv_all = lax.all_gather(kv_pair, "ctx", axis=0, tiled=True)
    doc_start = jnp.sum((segments < query_seg[0]).astype(jnp.int32))
    first_block = doc_start // rows_here
    attended = attend_window(queries, kv_all, query_seg, segments, my_block, first_block, group_size)
    slot_count = residual.shape[0]
    owner_count = lax.axis_size("tp")
    owners = owner_ids[:, 0]
    onehot = (owners[:, None] == jnp.arange(owner_count, dtype=jnp.int32)[None, :]).astype(
        jnp.int32
    )
    before = jnp.cumsum(onehot, axis=0) - onehot
    row_rank = jnp.sum(before * onehot, axis=1)
    slot_of_token = owners * slot_count + row_rank
    all_slots = jnp.arange(owner_count * slot_count, dtype=jnp.int32)
    select = (slot_of_token[None, :] == all_slots[:, None]).astype(jnp.bfloat16)
    attended_slots = jnp.dot(select, attended, preferred_element_type=jnp.float32).astype(
        jnp.bfloat16
    )
    partial_slots = jnp.dot(attended_slots, out_proj, preferred_element_type=jnp.float32).astype(
        jnp.bfloat16
    )
    owned_rows = lax.psum_scatter(partial_slots, "tp", scatter_dimension=0, tiled=True).astype(
        jnp.float32
    )
    hidden_sum = residual.astype(jnp.float32) + owned_rows
    mean_square = jnp.mean(hidden_sum * hidden_sum, axis=-1, keepdims=True)
    normed = hidden_sum * lax.rsqrt(mean_square + 1e-05) * norm_gain
    return (hidden_sum.astype(jnp.bfloat16), normed.astype(jnp.bfloat16))


def solution(mesh):
    placed = (
        P("ctx", "tp"),
        P("ctx", "tp"),
        P("ctx", "tp"),
        P(),
        P("ctx", None),
        P("tp", None),
        P(("ctx", "tp"), None),
        P(),
    )
    return jax.shard_map(
        on_device,
        mesh=mesh,
        in_specs=placed,
        out_specs=(P(("ctx", "tp"), None), P(("ctx", "tp"), None)),
        check_vma=False,
    )
```

```python
import functools
import math

import jax
import jax.numpy as jnp
from jax import lax
from jax.experimental import pallas as pl
from jax.experimental.pallas import tpu as pltpu
from jax.sharding import PartitionSpec as P

HEADS = 32
KV_HEADS = 8
HEAD_DIM = 128
DOC_MOST = 4096


def attention_kernel(
    block_info,
    qt_ref,
    kv_ref,
    kv_next_ref,
    qseg_ref,
    kseg_ref,
    kseg_next_ref,
    out_ref,
    max_ref,
    total_ref,
    acc_ref,
    *,
    window,
    group,
):
    step = pl.program_id(0)
    my_block = block_info[0]
    first_block = block_info[1]
    steps = (window + 1) // 2
    rows = qt_ref.shape[1] // group
    key_width = kv_ref.shape[0]
    local_heads = acc_ref.shape[0] * group
    kv_cols = kv_ref.shape[1] // 2
    score_scale = 1.0 / math.sqrt(HEAD_DIM)

    @pl.when(step == 0)
    def _():
        max_ref[...] = jnp.full(max_ref.shape, -1e29, jnp.float32)
        total_ref[...] = jnp.zeros(total_ref.shape, jnp.float32)
        acc_ref[...] = jnp.zeros(acc_ref.shape, jnp.float32)

    def accumulate(masked, kv_ref, kseg_ref, key_block):
        if masked:
            lane = lax.broadcasted_iota(jnp.int32, (1, group * rows), 1)
            query_pos = block_info[2] + lane % rows
            key_pos = key_block * key_width + lax.broadcasted_iota(jnp.int32, (key_width, 1), 0)
            allowed = (kseg_ref[...] == qseg_ref[...]) & (key_pos <= query_pos)
        for kv_head in range(local_heads // group):
            keys = kv_ref[:, kv_head * HEAD_DIM:(kv_head + 1) * HEAD_DIM]
            values = kv_ref[:, kv_cols + kv_head * HEAD_DIM:kv_cols + (kv_head + 1) * HEAD_DIM]
            values_t = values.astype(jnp.float32).T.astype(jnp.bfloat16)
            query_t = qt_ref[kv_head * HEAD_DIM:(kv_head + 1) * HEAD_DIM, :]
            scores = jnp.dot(keys, query_t, preferred_element_type=jnp.float32) * score_scale
            if masked:
                scores = jnp.where(allowed, scores, -1e30)
            running_max = max_ref[kv_head]
            new_max = jnp.maximum(running_max, jnp.max(scores, axis=0, keepdims=True))
            exponent = jnp.exp(scores - new_max)
            factor = jnp.exp(running_max - new_max)
            total_ref[kv_head] = total_ref[kv_head] * factor + jnp.sum(
                exponent, axis=0, keepdims=True
            )
            acc_ref[kv_head] = acc_ref[kv_head] * factor + jnp.dot(
                values_t, exponent.astype(jnp.bfloat16), preferred_element_type=jnp.float32
            )
            max_ref[kv_head] = new_max

    for sub, (kv_sub, kseg_sub) in enumerate(((kv_ref, kseg_ref), (kv_next_ref, kseg_next_ref))):
        place = 2 * step + sub
        key_block = my_block - (window - 1) + place
        active = (key_block >= first_block) & (place < window)
        whole = block_info[3 + place] == 1

        @pl.when(active & whole)
        def _():
            accumulate(False, kv_sub, kseg_sub, key_block)

        @pl.when(active & jnp.logical_not(whole))
        def _():
            accumulate(True, kv_sub, kseg_sub, key_block)

    @pl.when(step == steps - 1)
    def _():
        for head in range(local_heads):
            kv_head, member = divmod(head, group)
            lanes = slice(member * rows, (member + 1) * rows)
            mixed = acc_ref[kv_head, :, lanes] / total_ref[kv_head, :, lanes]
            out_ref[:, head * HEAD_DIM:(head + 1) * HEAD_DIM] = mixed.T.astype(out_ref.dtype)


def attend_window(queries, kv_all, query_seg, segments, my_block, first_block, group):
    rows, q_cols = queries.shape
    key_width = rows
    block_count = kv_all.shape[0] // key_width
    window = min(block_count, DOC_MOST // key_width + 1)
    local_heads = q_cols // HEAD_DIM
    kv_cols = kv_all.shape[1] // 2
    kv_local = local_heads // group
    queries_t = (
        queries.reshape(rows, kv_local, group, HEAD_DIM)
        .transpose(1, 3, 2, 0)
        .reshape(kv_local * HEAD_DIM, group * rows)
    )
    global_blocks = my_block - (window - 1) + jnp.arange(window, dtype=jnp.int32)
    clamped = jnp.clip(global_blocks, 0, block_count - 1)
    key_first = segments[clamped * key_width]
    key_last = segments[clamped * key_width + key_width - 1]
    whole = (
        (key_first == key_last)
        & (key_first == query_seg[0])
        & (query_seg[0] == query_seg[rows - 1])
        & (global_blocks < my_block)
        & (global_blocks >= 0)
    )
    steps = (window + 1) // 2
    block_info = jnp.concatenate(
        [
            jnp.stack([my_block, first_block, my_block * rows]),
            whole.astype(jnp.int32),
            jnp.zeros((2 * steps - window,), jnp.int32),
        ]
    ).astype(jnp.int32)

    def key_index(place, info):
        return jnp.minimum(jnp.maximum(info[0] - (window - 1) + place, info[1]), info[0])

    grid_spec = pltpu.PrefetchScalarGridSpec(
        num_scalar_prefetch=1,
        grid=(steps,),
        in_specs=[
            pl.BlockSpec((kv_cols, group * rows), lambda step, info: (0, 0)),
            pl.BlockSpec(
                (key_width, 2 * kv_cols), lambda step, info: (key_index(2 * step, info), 0)
            ),
            pl.BlockSpec(
                (key_width, 2 * kv_cols), lambda step, info: (key_index(2 * step + 1, info), 0)
            ),
            pl.BlockSpec((1, group * rows), lambda step, info: (0, 0)),
            pl.BlockSpec((key_width, 1), lambda step, info: (key_index(2 * step, info), 0)),
            pl.BlockSpec((key_width, 1), lambda step, info: (key_index(2 * step + 1, info), 0)),
        ],
        out_specs=pl.BlockSpec((rows, q_cols), lambda step, info: (0, 0)),
        scratch_shapes=[
            pltpu.VMEM((kv_local, 1, group * rows), jnp.float32),
            pltpu.VMEM((kv_local, 1, group * rows), jnp.float32),
            pltpu.VMEM((kv_local, HEAD_DIM, group * rows), jnp.float32),
        ],
    )
    kernel = pl.pallas_call(
        functools.partial(attention_kernel, window=window, group=group),
        grid_spec=grid_spec,
        out_shape=jax.ShapeDtypeStruct((rows, q_cols), jnp.bfloat16),
        compiler_params=pltpu.CompilerParams(dimension_semantics=("arbitrary",)),
    )
    attended_t = kernel(
        block_info,
        queries_t,
        kv_all,
        kv_all,
        jnp.tile(query_seg, group).reshape(1, group * rows),
        segments.reshape(-1, 1),
        segments.reshape(-1, 1),
    )
    return attended_t


def on_device(queries, key_rows, value_rows, segments, owner_ids, out_proj, residual, norm_gain):
    rows_here = queries.shape[0]
    kv_local = key_rows.shape[1] // HEAD_DIM
    kv_cols = kv_local * HEAD_DIM
    group_size = HEADS // KV_HEADS
    score_scale = 1.0 / math.sqrt(HEAD_DIM)
    my_block = lax.axis_index("ctx")
    my_start = my_block * rows_here
    query_heads = queries.reshape(rows_here, kv_local, group_size, HEAD_DIM)
    query_pos = my_start + jnp.arange(rows_here, dtype=jnp.int32)
    query_seg = lax.dynamic_slice_in_dim(segments, my_start, rows_here, 0)
    kv_pair = jnp.concatenate([key_rows, value_rows], axis=1)
    kv_all = lax.all_gather(kv_pair, "ctx", axis=0, tiled=True)
    doc_start = jnp.sum((segments < query_seg[0]).astype(jnp.int32))
    first_block = doc_start // rows_here
    attended = attend_window(queries, kv_all, query_seg, segments, my_block, first_block, group_size)
    slot_count = residual.shape[0]
    owner_count = lax.axis_size("tp")
    owners = owner_ids[:, 0]
    onehot = (owners[:, None] == jnp.arange(owner_count, dtype=jnp.int32)[None, :]).astype(
        jnp.int32
    )
    before = jnp.cumsum(onehot, axis=0) - onehot
    row_rank = jnp.sum(before * onehot, axis=1)
    slot_of_token = owners * slot_count + row_rank
    all_slots = jnp.arange(owner_count * slot_count, dtype=jnp.int32)
    select = (slot_of_token[None, :] == all_slots[:, None]).astype(jnp.bfloat16)
    attended_slots = jnp.dot(select, attended, preferred_element_type=jnp.float32).astype(
        jnp.bfloat16
    )
    partial_slots = jnp.dot(attended_slots, out_proj, preferred_element_type=jnp.float32).astype(
        jnp.bfloat16
    )
    owned_rows = lax.psum_scatter(partial_slots, "tp", scatter_dimension=0, tiled=True).astype(
        jnp.float32
    )
    hidden_sum = residual.astype(jnp.float32) + owned_rows
    mean_square = jnp.mean(hidden_sum * hidden_sum, axis=-1, keepdims=True)
    normed = hidden_sum * lax.rsqrt(mean_square + 1e-05) * norm_gain
    return (hidden_sum.astype(jnp.bfloat16), normed.astype(jnp.bfloat16))


def solution(mesh):
    placed = (
        P("ctx", "tp"),
        P("ctx", "tp"),
        P("ctx", "tp"),
        P(),
        P("ctx", None),
        P("tp", None),
        P(("ctx", "tp"), None),
        P(),
    )
    return jax.shard_map(
        on_device,
        mesh=mesh,
        in_specs=placed,
        out_specs=(P(("ctx", "tp"), None), P(("ctx", "tp"), None)),
        check_vma=False,
    )
```

```python
import functools
import math

import jax
import jax.numpy as jnp
from jax import lax
from jax.experimental import pallas as pl
from jax.experimental.pallas import tpu as pltpu
from jax.sharding import PartitionSpec as P

HEADS = 32
KV_HEADS = 8
HEAD_DIM = 128
DOC_MOST = 4096


def attention_kernel(
    block_info,
    qt_ref,
    kv_ref,
    kv_next_ref,
    qseg_ref,
    kseg_ref,
    kseg_next_ref,
    out_ref,
    max_ref,
    total_ref,
    acc_ref,
    *,
    window,
    group,
):
    step = pl.program_id(0)
    my_block = block_info[0]
    first_block = block_info[1]
    steps = (window + 1) // 2
    rows = qt_ref.shape[1] // group
    key_width = kv_ref.shape[0]
    local_heads = acc_ref.shape[0] * group
    kv_cols = kv_ref.shape[1] // 2
    score_scale = 1.0 / math.sqrt(HEAD_DIM)

    @pl.when(step == 0)
    def _():
        max_ref[...] = jnp.full(max_ref.shape, -1e29, jnp.float32)
        total_ref[...] = jnp.zeros(total_ref.shape, jnp.float32)
        acc_ref[...] = jnp.zeros(acc_ref.shape, jnp.float32)

    def accumulate(masked, kv_ref, kseg_ref, key_block):
        if masked:
            lane = lax.broadcasted_iota(jnp.int32, (1, group * rows), 1)
            query_pos = block_info[2] + lane % rows
            key_pos = key_block * key_width + lax.broadcasted_iota(jnp.int32, (key_width, 1), 0)
            allowed = (kseg_ref[...] == qseg_ref[...]) & (key_pos <= query_pos)
        for kv_head in range(local_heads // group):
            keys = kv_ref[:, kv_head * HEAD_DIM:(kv_head + 1) * HEAD_DIM]
            values = kv_ref[:, kv_cols + kv_head * HEAD_DIM:kv_cols + (kv_head + 1) * HEAD_DIM]
            values_t = values.astype(jnp.float32).T.astype(jnp.bfloat16)
            query_t = qt_ref[kv_head * HEAD_DIM:(kv_head + 1) * HEAD_DIM, :]
            scores = jnp.dot(keys, query_t, preferred_element_type=jnp.float32) * score_scale
            if masked:
                scores = jnp.where(allowed, scores, -1e30)
            running_max = max_ref[kv_head]
            new_max = jnp.maximum(running_max, jnp.max(scores, axis=0, keepdims=True))
            exponent = jnp.exp(scores - new_max)
            factor = jnp.exp(running_max - new_max)
            total_ref[kv_head] = total_ref[kv_head] * factor + jnp.sum(
                exponent, axis=0, keepdims=True
            )
            acc_ref[kv_head] = acc_ref[kv_head] * factor + jnp.dot(
                values_t, exponent.astype(jnp.bfloat16), preferred_element_type=jnp.float32
            )
            max_ref[kv_head] = new_max

    for sub, (kv_sub, kseg_sub) in enumerate(((kv_ref, kseg_ref), (kv_next_ref, kseg_next_ref))):
        place = 2 * step + sub
        key_block = my_block - (window - 1) + place
        active = (key_block >= first_block) & (place < window)
        whole = block_info[3 + place] == 1

        @pl.when(active & whole)
        def _():
            accumulate(False, kv_sub, kseg_sub, key_block)

        @pl.when(active & jnp.logical_not(whole))
        def _():
            accumulate(True, kv_sub, kseg_sub, key_block)

    @pl.when(step == steps - 1)
    def _():
        for head in range(local_heads):
            kv_head, member = divmod(head, group)
            lanes = slice(member * rows, (member + 1) * rows)
            mixed = acc_ref[kv_head, :, lanes] / total_ref[kv_head, :, lanes]
            out_ref[:, head * HEAD_DIM:(head + 1) * HEAD_DIM] = mixed.T.astype(out_ref.dtype)


def attend_window(queries, kv_all, query_seg, segments, my_block, first_block, group):
    rows, q_cols = queries.shape
    key_width = rows
    block_count = kv_all.shape[0] // key_width
    window = min(block_count, DOC_MOST // key_width + 1)
    local_heads = q_cols // HEAD_DIM
    kv_cols = kv_all.shape[1] // 2
    kv_local = local_heads // group
    queries_t = (
        queries.reshape(rows, kv_local, group, HEAD_DIM)
        .transpose(1, 3, 2, 0)
        .reshape(kv_local * HEAD_DIM, group * rows)
    )
    global_blocks = my_block - (window - 1) + jnp.arange(window, dtype=jnp.int32)
    clamped = jnp.clip(global_blocks, 0, block_count - 1)
    key_first = segments[clamped * key_width]
    key_last = segments[clamped * key_width + key_width - 1]
    whole = (
        (key_first == key_last)
        & (key_first == query_seg[0])
        & (query_seg[0] == query_seg[rows - 1])
        & (global_blocks < my_block)
        & (global_blocks >= 0)
    )
    steps = (window + 1) // 2
    block_info = jnp.concatenate(
        [
            jnp.stack([my_block, first_block, my_block * rows]),
            whole.astype(jnp.int32),
            jnp.zeros((2 * steps - window,), jnp.int32),
        ]
    ).astype(jnp.int32)

    def key_index(place, info):
        return jnp.minimum(jnp.maximum(info[0] - (window - 1) + place, info[1]), info[0])

    grid_spec = pltpu.PrefetchScalarGridSpec(
        num_scalar_prefetch=1,
        grid=(steps,),
        in_specs=[
            pl.BlockSpec((kv_cols, group * rows), lambda step, info: (0, 0)),
            pl.BlockSpec(
                (key_width, 2 * kv_cols), lambda step, info: (key_index(2 * step, info), 0)
            ),
            pl.BlockSpec(
                (key_width, 2 * kv_cols), lambda step, info: (key_index(2 * step + 1, info), 0)
            ),
            pl.BlockSpec((1, group * rows), lambda step, info: (0, 0)),
            pl.BlockSpec((key_width, 1), lambda step, info: (key_index(2 * step, info), 0)),
            pl.BlockSpec((key_width, 1), lambda step, info: (key_index(2 * step + 1, info), 0)),
        ],
        out_specs=pl.BlockSpec((rows, q_cols), lambda step, info: (0, 0)),
        scratch_shapes=[
            pltpu.VMEM((kv_local, 1, group * rows), jnp.float32),
            pltpu.VMEM((kv_local, 1, group * rows), jnp.float32),
            pltpu.VMEM((kv_local, HEAD_DIM, group * rows), jnp.float32),
        ],
    )
    kernel = pl.pallas_call(
        functools.partial(attention_kernel, window=window, group=group),
        grid_spec=grid_spec,
        out_shape=jax.ShapeDtypeStruct((rows, q_cols), jnp.bfloat16),
        compiler_params=pltpu.CompilerParams(dimension_semantics=("arbitrary",)),
    )
    attended_t = kernel(
        block_info,
        queries_t,
        kv_all,
        kv_all,
        jnp.tile(query_seg, group).reshape(1, group * rows),
        segments.reshape(-1, 1),
        segments.reshape(-1, 1),
    )
    return attended_t


def norm_kernel(residual_ref, rows_ref, gain_ref, hidden_ref, normed_ref):
    hidden_sum = residual_ref[...].astype(jnp.float32) + rows_ref[...].astype(jnp.float32)
    mean_square = jnp.mean(hidden_sum * hidden_sum, axis=-1, keepdims=True)
    normed = hidden_sum * lax.rsqrt(mean_square + 1e-05) * gain_ref[...]
    hidden_ref[...] = hidden_sum.astype(hidden_ref.dtype)
    normed_ref[...] = normed.astype(normed_ref.dtype)


def add_and_norm(residual, owned_rows, norm_gain):
    slot_count, width = residual.shape
    block_rows = 16 if slot_count % 16 == 0 else slot_count
    row_spec = pl.BlockSpec((block_rows, width), lambda step: (step, 0))
    return pl.pallas_call(
        norm_kernel,
        grid=(slot_count // block_rows,),
        in_specs=[row_spec, row_spec, pl.BlockSpec((1, width), lambda step: (0, 0))],
        out_specs=(row_spec, row_spec),
        out_shape=(
            jax.ShapeDtypeStruct((slot_count, width), jnp.bfloat16),
            jax.ShapeDtypeStruct((slot_count, width), jnp.bfloat16),
        ),
    )(residual, owned_rows, norm_gain.reshape(1, width))


def on_device(queries, key_rows, value_rows, segments, owner_ids, out_proj, residual, norm_gain):
    rows_here = queries.shape[0]
    kv_local = key_rows.shape[1] // HEAD_DIM
    kv_cols = kv_local * HEAD_DIM
    group_size = HEADS // KV_HEADS
    score_scale = 1.0 / math.sqrt(HEAD_DIM)
    my_block = lax.axis_index("ctx")
    my_start = my_block * rows_here
    query_heads = queries.reshape(rows_here, kv_local, group_size, HEAD_DIM)
    query_pos = my_start + jnp.arange(rows_here, dtype=jnp.int32)
    query_seg = lax.dynamic_slice_in_dim(segments, my_start, rows_here, 0)
    kv_pair = jnp.concatenate([key_rows, value_rows], axis=1)
    kv_all = lax.all_gather(kv_pair, "ctx", axis=0, tiled=True)
    doc_start = jnp.sum((segments < query_seg[0]).astype(jnp.int32))
    first_block = doc_start // rows_here
    attended = attend_window(queries, kv_all, query_seg, segments, my_block, first_block, group_size)
    slot_count = residual.shape[0]
    owner_count = lax.axis_size("tp")
    owners = owner_ids[:, 0]
    onehot = (owners[:, None] == jnp.arange(owner_count, dtype=jnp.int32)[None, :]).astype(
        jnp.int32
    )
    before = jnp.cumsum(onehot, axis=0) - onehot
    row_rank = jnp.sum(before * onehot, axis=1)
    slot_of_token = owners * slot_count + row_rank
    all_slots = jnp.arange(owner_count * slot_count, dtype=jnp.int32)
    select = (slot_of_token[None, :] == all_slots[:, None]).astype(jnp.bfloat16)
    attended_slots = jnp.dot(select, attended, preferred_element_type=jnp.float32).astype(
        jnp.bfloat16
    )
    partial_slots = jnp.dot(attended_slots, out_proj, preferred_element_type=jnp.float32).astype(
        jnp.bfloat16
    )
    owned_rows = lax.psum_scatter(partial_slots, "tp", scatter_dimension=0, tiled=True)
    return add_and_norm(residual, owned_rows, norm_gain)


def solution(mesh):
    placed = (
        P("ctx", "tp"),
        P("ctx", "tp"),
        P("ctx", "tp"),
        P(),
        P("ctx", None),
        P("tp", None),
        P(("ctx", "tp"), None),
        P(),
    )
    return jax.shard_map(
        on_device,
        mesh=mesh,
        in_specs=placed,
        out_specs=(P(("ctx", "tp"), None), P(("ctx", "tp"), None)),
        check_vma=False,
    )
```

```python
import functools
import math

import jax
import jax.numpy as jnp
from jax import lax
from jax.experimental import pallas as pl
from jax.experimental.pallas import tpu as pltpu
from jax.sharding import PartitionSpec as P

HEADS = 32
KV_HEADS = 8
HEAD_DIM = 128
DOC_MOST = 4096


def attention_kernel(
    block_info,
    qt_ref,
    kv_ref,
    kv_next_ref,
    qseg_ref,
    kseg_ref,
    kseg_next_ref,
    out_ref,
    max_ref,
    total_ref,
    acc_ref,
    *,
    window,
    group,
):
    step = pl.program_id(0)
    my_block = block_info[0]
    first_block = block_info[1]
    steps = (window + 1) // 2
    rows = qt_ref.shape[1] // group
    key_width = kv_ref.shape[0]
    local_heads = acc_ref.shape[0] * group
    kv_cols = kv_ref.shape[1] // 2
    score_scale = 1.0 / math.sqrt(HEAD_DIM)

    @pl.when(step == 0)
    def _():
        max_ref[...] = jnp.full(max_ref.shape, -1e29, jnp.float32)
        total_ref[...] = jnp.zeros(total_ref.shape, jnp.float32)
        acc_ref[...] = jnp.zeros(acc_ref.shape, jnp.float32)

    def accumulate(masked, kv_ref, kseg_ref, key_block):
        if masked:
            lane = lax.broadcasted_iota(jnp.int32, (1, group * rows), 1)
            query_pos = block_info[2] + lane % rows
            key_pos = key_block * key_width + lax.broadcasted_iota(jnp.int32, (key_width, 1), 0)
            allowed = (kseg_ref[...] == qseg_ref[...]) & (key_pos <= query_pos)
        for kv_head in range(local_heads // group):
            keys = kv_ref[:, kv_head * HEAD_DIM:(kv_head + 1) * HEAD_DIM]
            values = kv_ref[:, kv_cols + kv_head * HEAD_DIM:kv_cols + (kv_head + 1) * HEAD_DIM]
            values_t = values.astype(jnp.float32).T.astype(jnp.bfloat16)
            query_t = qt_ref[kv_head * HEAD_DIM:(kv_head + 1) * HEAD_DIM, :]
            scores = jnp.dot(keys, query_t, preferred_element_type=jnp.float32) * score_scale
            if masked:
                scores = jnp.where(allowed, scores, -1e30)
            running_max = max_ref[kv_head]
            new_max = jnp.maximum(running_max, jnp.max(scores, axis=0, keepdims=True))
            exponent = jnp.exp(scores - new_max)
            factor = jnp.exp(running_max - new_max)
            total_ref[kv_head] = total_ref[kv_head] * factor + jnp.sum(
                exponent, axis=0, keepdims=True
            )
            acc_ref[kv_head] = acc_ref[kv_head] * factor + jnp.dot(
                values_t, exponent.astype(jnp.bfloat16), preferred_element_type=jnp.float32
            )
            max_ref[kv_head] = new_max

    for sub, (kv_sub, kseg_sub) in enumerate(((kv_ref, kseg_ref), (kv_next_ref, kseg_next_ref))):
        place = 2 * step + sub
        key_block = my_block - (window - 1) + place
        active = (key_block >= first_block) & (place < window)
        whole = block_info[3 + place] == 1

        @pl.when(active & whole)
        def _():
            accumulate(False, kv_sub, kseg_sub, key_block)

        @pl.when(active & jnp.logical_not(whole))
        def _():
            accumulate(True, kv_sub, kseg_sub, key_block)

    @pl.when(step == steps - 1)
    def _():
        for head in range(local_heads):
            kv_head, member = divmod(head, group)
            lanes = slice(member * rows, (member + 1) * rows)
            mixed = acc_ref[kv_head, :, lanes] / total_ref[kv_head, :, lanes]
            out_ref[:, head * HEAD_DIM:(head + 1) * HEAD_DIM] = mixed.T.astype(out_ref.dtype)


def attend_window(queries, kv_all, query_seg, segments, my_block, first_block, group):
    rows, q_cols = queries.shape
    key_width = rows
    block_count = kv_all.shape[0] // key_width
    window = min(block_count, DOC_MOST // key_width + 1)
    local_heads = q_cols // HEAD_DIM
    kv_cols = kv_all.shape[1] // 2
    kv_local = local_heads // group
    queries_t = (
        queries.reshape(rows, kv_local, group, HEAD_DIM)
        .transpose(1, 3, 2, 0)
        .reshape(kv_local * HEAD_DIM, group * rows)
    )
    global_blocks = my_block - (window - 1) + jnp.arange(window, dtype=jnp.int32)
    clamped = jnp.clip(global_blocks, 0, block_count - 1)
    key_first = segments[clamped * key_width]
    key_last = segments[clamped * key_width + key_width - 1]
    whole = (
        (key_first == key_last)
        & (key_first == query_seg[0])
        & (query_seg[0] == query_seg[rows - 1])
        & (global_blocks < my_block)
        & (global_blocks >= 0)
    )
    steps = (window + 1) // 2
    block_info = jnp.concatenate(
        [
            jnp.stack([my_block, first_block, my_block * rows]),
            whole.astype(jnp.int32),
            jnp.zeros((2 * steps - window,), jnp.int32),
        ]
    ).astype(jnp.int32)

    def key_index(place, info):
        return jnp.minimum(jnp.maximum(info[0] - (window - 1) + place, info[1]), info[0])

    grid_spec = pltpu.PrefetchScalarGridSpec(
        num_scalar_prefetch=1,
        grid=(steps,),
        in_specs=[
            pl.BlockSpec((kv_cols, group * rows), lambda step, info: (0, 0)),
            pl.BlockSpec(
                (key_width, 2 * kv_cols), lambda step, info: (key_index(2 * step, info), 0)
            ),
            pl.BlockSpec(
                (key_width, 2 * kv_cols), lambda step, info: (key_index(2 * step + 1, info), 0)
            ),
            pl.BlockSpec((1, group * rows), lambda step, info: (0, 0)),
            pl.BlockSpec((key_width, 1), lambda step, info: (key_index(2 * step, info), 0)),
            pl.BlockSpec((key_width, 1), lambda step, info: (key_index(2 * step + 1, info), 0)),
        ],
        out_specs=pl.BlockSpec((rows, q_cols), lambda step, info: (0, 0)),
        scratch_shapes=[
            pltpu.VMEM((kv_local, 1, group * rows), jnp.float32),
            pltpu.VMEM((kv_local, 1, group * rows), jnp.float32),
            pltpu.VMEM((kv_local, HEAD_DIM, group * rows), jnp.float32),
        ],
    )
    kernel = pl.pallas_call(
        functools.partial(attention_kernel, window=window, group=group),
        grid_spec=grid_spec,
        out_shape=jax.ShapeDtypeStruct((rows, q_cols), jnp.bfloat16),
        compiler_params=pltpu.CompilerParams(dimension_semantics=("arbitrary",)),
    )
    attended_t = kernel(
        block_info,
        queries_t,
        kv_all,
        kv_all,
        jnp.tile(query_seg, group).reshape(1, group * rows),
        segments.reshape(-1, 1),
        segments.reshape(-1, 1),
    )
    return attended_t


def on_device(queries, key_rows, value_rows, segments, owner_ids, out_proj, residual, norm_gain):
    rows_here = queries.shape[0]
    kv_local = key_rows.shape[1] // HEAD_DIM
    kv_cols = kv_local * HEAD_DIM
    group_size = HEADS // KV_HEADS
    score_scale = 1.0 / math.sqrt(HEAD_DIM)
    my_block = lax.axis_index("ctx")
    my_start = my_block * rows_here
    query_heads = queries.reshape(rows_here, kv_local, group_size, HEAD_DIM)
    query_pos = my_start + jnp.arange(rows_here, dtype=jnp.int32)
    query_seg = lax.dynamic_slice_in_dim(segments, my_start, rows_here, 0)
    kv_pair = jnp.concatenate([key_rows, value_rows], axis=1)
    kv_all = lax.all_gather(kv_pair, "ctx", axis=0, tiled=True)
    doc_start = jnp.sum((segments < query_seg[0]).astype(jnp.int32))
    first_block = doc_start // rows_here
    attended = attend_window(queries, kv_all, query_seg, segments, my_block, first_block, group_size)
    slot_count = residual.shape[0]
    owner_count = lax.axis_size("tp")
    owners = owner_ids[:, 0]
    onehot = (owners[:, None] == jnp.arange(owner_count, dtype=jnp.int32)[None, :]).astype(
        jnp.int32
    )
    before = jnp.cumsum(onehot, axis=0) - onehot
    row_rank = jnp.sum(before * onehot, axis=1)
    slot_of_token = owners * slot_count + row_rank
    all_slots = jnp.arange(owner_count * slot_count, dtype=jnp.int32)
    select = (slot_of_token[None, :] == all_slots[:, None]).astype(jnp.bfloat16)
    attended_slots = jnp.dot(select, attended, preferred_element_type=jnp.float32).astype(
        jnp.bfloat16
    )
    attended_slots = lax.optimization_barrier(attended_slots)
    partial_slots = jnp.dot(attended_slots, out_proj, preferred_element_type=jnp.float32).astype(
        jnp.bfloat16
    )
    owned_rows = lax.psum_scatter(partial_slots, "tp", scatter_dimension=0, tiled=True).astype(
        jnp.float32
    )
    hidden_sum = residual.astype(jnp.float32) + owned_rows
    mean_square = jnp.mean(hidden_sum * hidden_sum, axis=-1, keepdims=True)
    normed = hidden_sum * lax.rsqrt(mean_square + 1e-05) * norm_gain
    return (hidden_sum.astype(jnp.bfloat16), normed.astype(jnp.bfloat16))


def solution(mesh):
    placed = (
        P("ctx", "tp"),
        P("ctx", "tp"),
        P("ctx", "tp"),
        P(),
        P("ctx", None),
        P("tp", None),
        P(("ctx", "tp"), None),
        P(),
    )
    return jax.shard_map(
        on_device,
        mesh=mesh,
        in_specs=placed,
        out_specs=(P(("ctx", "tp"), None), P(("ctx", "tp"), None)),
        check_vma=False,
    )
```

```python
import functools
import math

import jax
import jax.numpy as jnp
from jax import lax
from jax.experimental import pallas as pl
from jax.experimental.pallas import tpu as pltpu
from jax.sharding import PartitionSpec as P

HEADS = 32
KV_HEADS = 8
HEAD_DIM = 128
DOC_MOST = 4096
PER_STEP = 3


def attention_kernel(
    block_info,
    qt_ref,
    *refs,
    window,
    group,
):
    kv_refs = refs[:PER_STEP]
    qseg_ref = refs[PER_STEP]
    kseg_refs = refs[PER_STEP + 1:2 * PER_STEP + 1]
    out_ref, max_ref, total_ref, acc_ref = refs[2 * PER_STEP + 1:]
    kv_ref = kv_refs[0]
    step = pl.program_id(0)
    my_block = block_info[0]
    first_block = block_info[1]
    steps = -(-window // PER_STEP)
    rows = qt_ref.shape[1] // group
    key_width = kv_ref.shape[0]
    local_heads = acc_ref.shape[0] * group
    kv_cols = kv_ref.shape[1] // 2
    score_scale = 1.0 / math.sqrt(HEAD_DIM)

    @pl.when(step == 0)
    def _():
        max_ref[...] = jnp.full(max_ref.shape, -1e29, jnp.float32)
        total_ref[...] = jnp.zeros(total_ref.shape, jnp.float32)
        acc_ref[...] = jnp.zeros(acc_ref.shape, jnp.float32)

    def accumulate(masked, kv_ref, kseg_ref, key_block):
        if masked:
            lane = lax.broadcasted_iota(jnp.int32, (1, group * rows), 1)
            query_pos = block_info[2] + lane % rows
            key_pos = key_block * key_width + lax.broadcasted_iota(jnp.int32, (key_width, 1), 0)
            allowed = (kseg_ref[...] == qseg_ref[...]) & (key_pos <= query_pos)
        for kv_head in range(local_heads // group):
            keys = kv_ref[:, kv_head * HEAD_DIM:(kv_head + 1) * HEAD_DIM]
            values = kv_ref[:, kv_cols + kv_head * HEAD_DIM:kv_cols + (kv_head + 1) * HEAD_DIM]
            values_t = values.astype(jnp.float32).T.astype(jnp.bfloat16)
            query_t = qt_ref[kv_head * HEAD_DIM:(kv_head + 1) * HEAD_DIM, :]
            scores = jnp.dot(keys, query_t, preferred_element_type=jnp.float32) * score_scale
            if masked:
                scores = jnp.where(allowed, scores, -1e30)
            running_max = max_ref[kv_head]
            new_max = jnp.maximum(running_max, jnp.max(scores, axis=0, keepdims=True))
            exponent = jnp.exp(scores - new_max)
            factor = jnp.exp(running_max - new_max)
            total_ref[kv_head] = total_ref[kv_head] * factor + jnp.sum(
                exponent, axis=0, keepdims=True
            )
            acc_ref[kv_head] = acc_ref[kv_head] * factor + jnp.dot(
                values_t, exponent.astype(jnp.bfloat16), preferred_element_type=jnp.float32
            )
            max_ref[kv_head] = new_max

    for sub, (kv_sub, kseg_sub) in enumerate(zip(kv_refs, kseg_refs)):
        place = PER_STEP * step + sub
        key_block = my_block - (window - 1) + place
        active = (key_block >= first_block) & (place < window)
        whole = block_info[3 + place] == 1

        @pl.when(active & whole)
        def _():
            accumulate(False, kv_sub, kseg_sub, key_block)

        @pl.when(active & jnp.logical_not(whole))
        def _():
            accumulate(True, kv_sub, kseg_sub, key_block)

    @pl.when(step == steps - 1)
    def _():
        for head in range(local_heads):
            kv_head, member = divmod(head, group)
            lanes = slice(member * rows, (member + 1) * rows)
            mixed = acc_ref[kv_head, :, lanes] / total_ref[kv_head, :, lanes]
            out_ref[:, head * HEAD_DIM:(head + 1) * HEAD_DIM] = mixed.T.astype(out_ref.dtype)


def attend_window(queries, kv_all, query_seg, segments, my_block, first_block, group):
    rows, q_cols = queries.shape
    key_width = rows
    block_count = kv_all.shape[0] // key_width
    window = min(block_count, DOC_MOST // key_width + 1)
    local_heads = q_cols // HEAD_DIM
    kv_cols = kv_all.shape[1] // 2
    kv_local = local_heads // group
    queries_t = (
        queries.reshape(rows, kv_local, group, HEAD_DIM)
        .transpose(1, 3, 2, 0)
        .reshape(kv_local * HEAD_DIM, group * rows)
    )
    global_blocks = my_block - (window - 1) + jnp.arange(window, dtype=jnp.int32)
    clamped = jnp.clip(global_blocks, 0, block_count - 1)
    key_first = segments[clamped * key_width]
    key_last = segments[clamped * key_width + key_width - 1]
    whole = (
        (key_first == key_last)
        & (key_first == query_seg[0])
        & (query_seg[0] == query_seg[rows - 1])
        & (global_blocks < my_block)
        & (global_blocks >= 0)
    )
    steps = -(-window // PER_STEP)
    block_info = jnp.concatenate(
        [
            jnp.stack([my_block, first_block, my_block * rows]),
            whole.astype(jnp.int32),
            jnp.zeros((PER_STEP * steps - window,), jnp.int32),
        ]
    ).astype(jnp.int32)

    def key_index(place, info):
        return jnp.minimum(jnp.maximum(info[0] - (window - 1) + place, info[1]), info[0])

    grid_spec = pltpu.PrefetchScalarGridSpec(
        num_scalar_prefetch=1,
        grid=(steps,),
        in_specs=[pl.BlockSpec((kv_cols, group * rows), lambda step, info: (0, 0))]
        + [
            pl.BlockSpec(
                (key_width, 2 * kv_cols),
                functools.partial(lambda sub, step, info: (key_index(PER_STEP * step + sub, info), 0), sub),
            )
            for sub in range(PER_STEP)
        ]
        + [pl.BlockSpec((1, group * rows), lambda step, info: (0, 0))]
        + [
            pl.BlockSpec(
                (key_width, 1),
                functools.partial(lambda sub, step, info: (key_index(PER_STEP * step + sub, info), 0), sub),
            )
            for sub in range(PER_STEP)
        ],
        out_specs=pl.BlockSpec((rows, q_cols), lambda step, info: (0, 0)),
        scratch_shapes=[
            pltpu.VMEM((kv_local, 1, group * rows), jnp.float32),
            pltpu.VMEM((kv_local, 1, group * rows), jnp.float32),
            pltpu.VMEM((kv_local, HEAD_DIM, group * rows), jnp.float32),
        ],
    )
    kernel = pl.pallas_call(
        functools.partial(attention_kernel, window=window, group=group),
        grid_spec=grid_spec,
        out_shape=jax.ShapeDtypeStruct((rows, q_cols), jnp.bfloat16),
        compiler_params=pltpu.CompilerParams(dimension_semantics=("arbitrary",)),
    )
    attended_t = kernel(
        block_info,
        queries_t,
        *([kv_all] * PER_STEP),
        jnp.tile(query_seg, group).reshape(1, group * rows),
        *([segments.reshape(-1, 1)] * PER_STEP),
    )
    return attended_t


def on_device(queries, key_rows, value_rows, segments, owner_ids, out_proj, residual, norm_gain):
    rows_here = queries.shape[0]
    kv_local = key_rows.shape[1] // HEAD_DIM
    kv_cols = kv_local * HEAD_DIM
    group_size = HEADS // KV_HEADS
    score_scale = 1.0 / math.sqrt(HEAD_DIM)
    my_block = lax.axis_index("ctx")
    my_start = my_block * rows_here
    query_heads = queries.reshape(rows_here, kv_local, group_size, HEAD_DIM)
    query_pos = my_start + jnp.arange(rows_here, dtype=jnp.int32)
    query_seg = lax.dynamic_slice_in_dim(segments, my_start, rows_here, 0)
    kv_pair = jnp.concatenate([key_rows, value_rows], axis=1)
    kv_all = lax.all_gather(kv_pair, "ctx", axis=0, tiled=True)
    doc_start = jnp.sum((segments < query_seg[0]).astype(jnp.int32))
    first_block = doc_start // rows_here
    attended = attend_window(queries, kv_all, query_seg, segments, my_block, first_block, group_size)
    slot_count = residual.shape[0]
    owner_count = lax.axis_size("tp")
    owners = owner_ids[:, 0]
    onehot = (owners[:, None] == jnp.arange(owner_count, dtype=jnp.int32)[None, :]).astype(
        jnp.int32
    )
    before = jnp.cumsum(onehot, axis=0) - onehot
    row_rank = jnp.sum(before * onehot, axis=1)
    slot_of_token = owners * slot_count + row_rank
    all_slots = jnp.arange(owner_count * slot_count, dtype=jnp.int32)
    select = (slot_of_token[None, :] == all_slots[:, None]).astype(jnp.bfloat16)
    attended_slots = jnp.dot(select, attended, preferred_element_type=jnp.float32).astype(
        jnp.bfloat16
    )
    partial_slots = jnp.dot(attended_slots, out_proj, preferred_element_type=jnp.float32).astype(
        jnp.bfloat16
    )
    owned_rows = lax.psum_scatter(partial_slots, "tp", scatter_dimension=0, tiled=True).astype(
        jnp.float32
    )
    hidden_sum = residual.astype(jnp.float32) + owned_rows
    mean_square = jnp.mean(hidden_sum * hidden_sum, axis=-1, keepdims=True)
    normed = hidden_sum * lax.rsqrt(mean_square + 1e-05) * norm_gain
    return (hidden_sum.astype(jnp.bfloat16), normed.astype(jnp.bfloat16))


def solution(mesh):
    placed = (
        P("ctx", "tp"),
        P("ctx", "tp"),
        P("ctx", "tp"),
        P(),
        P("ctx", None),
        P("tp", None),
        P(("ctx", "tp"), None),
        P(),
    )
    return jax.shard_map(
        on_device,
        mesh=mesh,
        in_specs=placed,
        out_specs=(P(("ctx", "tp"), None), P(("ctx", "tp"), None)),
        check_vma=False,
    )
```

```python
import functools
import math

import jax
import jax.numpy as jnp
from jax import lax
from jax.experimental import pallas as pl
from jax.experimental.pallas import tpu as pltpu
from jax.sharding import PartitionSpec as P

HEADS = 32
KV_HEADS = 8
HEAD_DIM = 128
DOC_MOST = 4096


def attention_kernel(
    block_info,
    qt_ref,
    kv_ref,
    kv_next_ref,
    qseg_ref,
    kseg_ref,
    kseg_next_ref,
    out_ref,
    max_ref,
    total_ref,
    acc_ref,
    *,
    window,
    group,
):
    step = pl.program_id(0)
    my_block = block_info[0]
    first_block = block_info[1]
    steps = (window + 1) // 2
    rows = qt_ref.shape[1] // group
    key_width = kv_ref.shape[0] // 2
    local_heads = acc_ref.shape[0] * group
    score_scale = 1.0 / math.sqrt(HEAD_DIM)

    @pl.when(step == 0)
    def _():
        max_ref[...] = jnp.full(max_ref.shape, -1e29, jnp.float32)
        total_ref[...] = jnp.zeros(total_ref.shape, jnp.float32)
        acc_ref[...] = jnp.zeros(acc_ref.shape, jnp.float32)

    def accumulate(masked, kv_ref, kseg_ref, key_block):
        if masked:
            lane = lax.broadcasted_iota(jnp.int32, (1, group * rows), 1)
            query_pos = block_info[2] + lane % rows
            key_pos = key_block * key_width + lax.broadcasted_iota(jnp.int32, (key_width, 1), 0)
            allowed = (kseg_ref[...] == qseg_ref[...]) & (key_pos <= query_pos)
        for kv_head in range(local_heads // group):
            keys = kv_ref[:key_width, kv_head * HEAD_DIM:(kv_head + 1) * HEAD_DIM]
            values = kv_ref[key_width:, kv_head * HEAD_DIM:(kv_head + 1) * HEAD_DIM]
            values_t = values.astype(jnp.float32).T.astype(jnp.bfloat16)
            query_t = qt_ref[kv_head * HEAD_DIM:(kv_head + 1) * HEAD_DIM, :]
            scores = jnp.dot(keys, query_t, preferred_element_type=jnp.float32) * score_scale
            if masked:
                scores = jnp.where(allowed, scores, -1e30)
            running_max = max_ref[kv_head]
            new_max = jnp.maximum(running_max, jnp.max(scores, axis=0, keepdims=True))
            exponent = jnp.exp(scores - new_max)
            factor = jnp.exp(running_max - new_max)
            total_ref[kv_head] = total_ref[kv_head] * factor + jnp.sum(
                exponent, axis=0, keepdims=True
            )
            acc_ref[kv_head] = acc_ref[kv_head] * factor + jnp.dot(
                values_t, exponent.astype(jnp.bfloat16), preferred_element_type=jnp.float32
            )
            max_ref[kv_head] = new_max

    for sub, (kv_sub, kseg_sub) in enumerate(((kv_ref, kseg_ref), (kv_next_ref, kseg_next_ref))):
        place = 2 * step + sub
        key_block = my_block - (window - 1) + place
        active = (key_block >= first_block) & (place < window)
        whole = block_info[3 + place] == 1

        @pl.when(active & whole)
        def _():
            accumulate(False, kv_sub, kseg_sub, key_block)

        @pl.when(active & jnp.logical_not(whole))
        def _():
            accumulate(True, kv_sub, kseg_sub, key_block)

    @pl.when(step == steps - 1)
    def _():
        for head in range(local_heads):
            kv_head, member = divmod(head, group)
            lanes = slice(member * rows, (member + 1) * rows)
            mixed = acc_ref[kv_head, :, lanes] / total_ref[kv_head, :, lanes]
            out_ref[:, head * HEAD_DIM:(head + 1) * HEAD_DIM] = mixed.T.astype(out_ref.dtype)


def attend_window(queries, kv_all, query_seg, segments, my_block, first_block, group):
    rows, q_cols = queries.shape
    key_width = rows
    block_count = kv_all.shape[0] // (2 * key_width)
    window = min(block_count, DOC_MOST // key_width + 1)
    local_heads = q_cols // HEAD_DIM
    kv_cols = kv_all.shape[1]
    kv_local = local_heads // group
    queries_t = (
        queries.reshape(rows, kv_local, group, HEAD_DIM)
        .transpose(1, 3, 2, 0)
        .reshape(kv_local * HEAD_DIM, group * rows)
    )
    global_blocks = my_block - (window - 1) + jnp.arange(window, dtype=jnp.int32)
    clamped = jnp.clip(global_blocks, 0, block_count - 1)
    key_first = segments[clamped * key_width]
    key_last = segments[clamped * key_width + key_width - 1]
    whole = (
        (key_first == key_last)
        & (key_first == query_seg[0])
        & (query_seg[0] == query_seg[rows - 1])
        & (global_blocks < my_block)
        & (global_blocks >= 0)
    )
    steps = (window + 1) // 2
    block_info = jnp.concatenate(
        [
            jnp.stack([my_block, first_block, my_block * rows]),
            whole.astype(jnp.int32),
            jnp.zeros((2 * steps - window,), jnp.int32),
        ]
    ).astype(jnp.int32)

    def key_index(place, info):
        return jnp.minimum(jnp.maximum(info[0] - (window - 1) + place, info[1]), info[0])

    grid_spec = pltpu.PrefetchScalarGridSpec(
        num_scalar_prefetch=1,
        grid=(steps,),
        in_specs=[
            pl.BlockSpec((kv_cols, group * rows), lambda step, info: (0, 0)),
            pl.BlockSpec(
                (2 * key_width, kv_cols), lambda step, info: (key_index(2 * step, info), 0)
            ),
            pl.BlockSpec(
                (2 * key_width, kv_cols), lambda step, info: (key_index(2 * step + 1, info), 0)
            ),
            pl.BlockSpec((1, group * rows), lambda step, info: (0, 0)),
            pl.BlockSpec((key_width, 1), lambda step, info: (key_index(2 * step, info), 0)),
            pl.BlockSpec((key_width, 1), lambda step, info: (key_index(2 * step + 1, info), 0)),
        ],
        out_specs=pl.BlockSpec((rows, q_cols), lambda step, info: (0, 0)),
        scratch_shapes=[
            pltpu.VMEM((kv_local, 1, group * rows), jnp.float32),
            pltpu.VMEM((kv_local, 1, group * rows), jnp.float32),
            pltpu.VMEM((kv_local, HEAD_DIM, group * rows), jnp.float32),
        ],
    )
    kernel = pl.pallas_call(
        functools.partial(attention_kernel, window=window, group=group),
        grid_spec=grid_spec,
        out_shape=jax.ShapeDtypeStruct((rows, q_cols), jnp.bfloat16),
        compiler_params=pltpu.CompilerParams(dimension_semantics=("arbitrary",)),
    )
    attended_t = kernel(
        block_info,
        queries_t,
        kv_all,
        kv_all,
        jnp.tile(query_seg, group).reshape(1, group * rows),
        segments.reshape(-1, 1),
        segments.reshape(-1, 1),
    )
    return attended_t


def on_device(queries, key_rows, value_rows, segments, owner_ids, out_proj, residual, norm_gain):
    rows_here = queries.shape[0]
    kv_local = key_rows.shape[1] // HEAD_DIM
    kv_cols = kv_local * HEAD_DIM
    group_size = HEADS // KV_HEADS
    score_scale = 1.0 / math.sqrt(HEAD_DIM)
    my_block = lax.axis_index("ctx")
    my_start = my_block * rows_here
    query_heads = queries.reshape(rows_here, kv_local, group_size, HEAD_DIM)
    query_pos = my_start + jnp.arange(rows_here, dtype=jnp.int32)
    query_seg = lax.dynamic_slice_in_dim(segments, my_start, rows_here, 0)
    kv_pair = jnp.concatenate([key_rows, value_rows], axis=0)
    kv_all = lax.all_gather(kv_pair, "ctx", axis=0, tiled=True)
    doc_start = jnp.sum((segments < query_seg[0]).astype(jnp.int32))
    first_block = doc_start // rows_here
    attended = attend_window(queries, kv_all, query_seg, segments, my_block, first_block, group_size)
    slot_count = residual.shape[0]
    owner_count = lax.axis_size("tp")
    owners = owner_ids[:, 0]
    onehot = (owners[:, None] == jnp.arange(owner_count, dtype=jnp.int32)[None, :]).astype(
        jnp.int32
    )
    before = jnp.cumsum(onehot, axis=0) - onehot
    row_rank = jnp.sum(before * onehot, axis=1)
    slot_of_token = owners * slot_count + row_rank
    all_slots = jnp.arange(owner_count * slot_count, dtype=jnp.int32)
    select = (slot_of_token[None, :] == all_slots[:, None]).astype(jnp.bfloat16)
    attended_slots = jnp.dot(select, attended, preferred_element_type=jnp.float32).astype(
        jnp.bfloat16
    )
    partial_slots = jnp.dot(attended_slots, out_proj, preferred_element_type=jnp.float32).astype(
        jnp.bfloat16
    )
    owned_rows = lax.psum_scatter(partial_slots, "tp", scatter_dimension=0, tiled=True).astype(
        jnp.float32
    )
    hidden_sum = residual.astype(jnp.float32) + owned_rows
    mean_square = jnp.mean(hidden_sum * hidden_sum, axis=-1, keepdims=True)
    normed = hidden_sum * lax.rsqrt(mean_square + 1e-05) * norm_gain
    return (hidden_sum.astype(jnp.bfloat16), normed.astype(jnp.bfloat16))


def solution(mesh):
    placed = (
        P("ctx", "tp"),
        P("ctx", "tp"),
        P("ctx", "tp"),
        P(),
        P("ctx", None),
        P("tp", None),
        P(("ctx", "tp"), None),
        P(),
    )
    return jax.shard_map(
        on_device,
        mesh=mesh,
        in_specs=placed,
        out_specs=(P(("ctx", "tp"), None), P(("ctx", "tp"), None)),
        check_vma=False,
    )
```
